512 devices in a mesh: seq: 64 (over z, x, core), head: 8 (over y).
Axes of the slice: x: 4, y: 8, z: 8, core: 2. Of those that a mesh axis runs over, the one named last changes fastest.
Arguments:
- projected: float32 [65536, 2560], P(('seq', 'head')), may hold values from -6 to 6
- out_grads: float32 [65536, 2048], P(('seq', 'head')), may hold values from -6 to 6
- conv_weight: float32 [3, 2560], replicated, may hold values from -2.4 to 2.4
- doc_lengths: int32 [16], replicated, may hold values from 1 to 32768, 65536 in all
Outputs:
- grad_projected: float32 [65536, 2560], P(('seq', 'head'))
- grad_conv: float32 [3, 2560], replicated
The draws below stay inside these ranges and needn't reach their ends.
Inputs may be any that keep to these rules, and one draw needn't show every extreme that they name: `doc_lengths`: the 16 documents fill the 65536 tokens end to end; the longest holds exactly half of 65536 tokens.
All inputs are finite; a program needn't handle non-finite values.
Results may differ from the reference program's by a relative error of at most 0.0003.
Values sent between devices are 32-bit elements; how exact they have to be, the bound alone decides.
No kernel may reach another device: no remote copies, remote signals or barrier semaphores. Data moves between devices by JAX's collectives and lax.ppermute only.
A program may use at most 128 MiB of HBM per device.

```python
import math
import jax
import jax.numpy as jnp
import numpy as np
from jax import lax

HEADS = 16
KEY_DIM = 16
HEAD_DIM = 128
CONV_TAPS = 3
TOKENS = 65536
NDOC = 16


def levels(own_key, dims, shards, low, top_value):
    gain = 1.0
    for axis_at, shards_of in shards:
        steps = jax.random.uniform(jax.random.fold_in(jax.random.fold_in(own_key, 6), axis_at), (shards_of,), jnp.float32, low / len(shards), top_value / len(shards))
        gain = gain * jnp.repeat(jnp.exp(steps), dims[axis_at] // shards_of).reshape((-1,) + (1,) * (len(dims) - 1 - axis_at))
    return gain


def split_up(count, total, limit, skew):
    loads = [(1 << 20) // math.isqrt(rank ** skew) + 1 for rank in range(2, count + 1)]
    rest, counts = total - limit - (count - 1), [1] * (count - 1)
    while rest > 0:
        movable = [i for i in range(count - 1) if counts[i] < limit]
        pool, remaining = sum([loads[i] for i in movable]), rest
        for i in movable:
            more = min(limit - counts[i], max(1, remaining * loads[i] // pool), rest)
            counts[i] = counts[i] + more
            rest = rest - more
    return np.array([limit] + counts)


def ragged_sizes(own_key, count, total, bound, slope):
    if count == 2:
        one = jax.random.randint(own_key, (), max(1, total - bound), min(bound, total - 1) + 1)
        return jnp.stack([one, total - one])
    lengths = jnp.asarray(split_up(count, total, bound, slope), jnp.int32)
    twos = (count - 1) // 2
    giver, receiver = lengths[1:1 + 2 * twos:2], lengths[2:2 + 2 * twos:2]
    margin = jnp.minimum(giver - 1, bound - receiver)
    shifted = jax.random.randint(jax.random.fold_in(own_key, 1), (twos,), 0, 1 << 20) % (margin + 1)
    lengths = lengths.at[1:1 + 2 * twos:2].set(giver - shifted).at[2:2 + 2 * twos:2].set(receiver + shifted)
    return lengths[jax.random.permutation(jax.random.fold_in(own_key, 2), count)]


def scatter_about(rng, shape, scale, bound, split=(), kind=jnp.bfloat16):
    entries = jax.random.normal(rng, shape, jnp.float32) * scale
    if len(split) > 0:
        entries = levels(rng, shape, split, -0.22, 0.18) * entries
    return jnp.clip(entries, min=-bound, max=bound).astype(kind)


def setup_inputs(seed: int = 0) -> dict:
    splits = jax.random.split(jax.random.key(seed), 5)
    projected = scatter_about(splits[0], (TOKENS, HEADS * (2 * KEY_DIM + HEAD_DIM)), 1.0, 6.0, ((0, 512),), jnp.float32)
    out_grads = scatter_about(splits[1], (TOKENS, HEADS * HEAD_DIM), 1.0, 6.0, ((0, 512),), jnp.float32)
    conv_weight = scatter_about(splits[2], (CONV_TAPS, HEADS * (2 * KEY_DIM + HEAD_DIM)), 0.6, 2.4, (), jnp.float32)
    doc_lengths = ragged_sizes(splits[3], NDOC, TOKENS, TOKENS // 2, 2).astype(jnp.int32)
    return dict(projected=projected, out_grads=out_grads, conv_weight=conv_weight, doc_lengths=doc_lengths)


HIGHEST = lax.Precision.HIGHEST

def feature_rows(matrix):
    key_size = matrix.shape[-1]
    upper_i, upper_j = np.triu_indices(key_size)
    factors = np.where(upper_i == upper_j, 1.0 / math.sqrt(2.0), 1.0)
    products = matrix[:, upper_i] * matrix[:, upper_j] * jnp.asarray(factors, dtype=jnp.float32)[None, :]
    constant = jnp.ones((matrix.shape[0], 1), jnp.float32)
    return jnp.concatenate([constant, matrix, products], axis=1)

def shift_rows(matrix, amount):
    return jnp.concatenate([jnp.zeros_like(matrix[:amount]), matrix[:-amount]], axis=0)

def head_attention(triple, begins):
    query_rows, key_rows, value_rows = triple
    total = query_rows.shape[0]
    span_len = 128
    pieces = total // span_len
    query_feat = feature_rows(query_rows)
    key_feat = feature_rows(key_rows)
    causal = jnp.arange(span_len)[:, None] >= jnp.arange(span_len)[None, :]

    def advance(carried, inputs):
        carry_state, carry_norm = carried
        query_blk, key_blk, value_blk, doc_blk, block_start = inputs
        allowed = (causal & (doc_blk[:, None] == doc_blk[None, :])).astype(jnp.float32)
        scores = jnp.dot(query_blk, key_blk.T, precision=HIGHEST) * allowed
        from_carry = (doc_blk < block_start).astype(jnp.float32)
        numerator = jnp.dot(scores, value_blk, precision=HIGHEST) + from_carry[:, None] * jnp.dot(query_blk, carry_state, precision=HIGHEST)
        denominator = lax.optimization_barrier(jnp.sum(scores, axis=1)) + from_carry * jnp.dot(query_blk, carry_norm, precision=HIGHEST)
        block_tail = (doc_blk == doc_blk[span_len - 1]).astype(jnp.float32)
        carry_keep = (doc_blk[span_len - 1] < block_start).astype(jnp.float32)
        tail_keys = key_blk * block_tail[:, None]
        next_state = jnp.dot(tail_keys.T, value_blk, precision=HIGHEST) + carry_keep * carry_state
        next_norm = lax.optimization_barrier(jnp.sum(tail_keys, axis=0)) + carry_keep * carry_norm
        return ((next_state, next_norm), numerator / denominator[:, None])
    stacked = (query_feat.reshape(pieces, span_len, -1), key_feat.reshape(pieces, span_len, -1), value_rows.reshape(pieces, span_len, -1), begins.reshape(pieces, span_len), (jnp.arange(pieces, dtype=jnp.int32) * span_len).astype(jnp.int32))
    initial = (jnp.zeros((query_feat.shape[1], value_rows.shape[1]), jnp.float32), jnp.zeros((query_feat.shape[1],), jnp.float32))
    swept_back = lax.scan(jax.checkpoint(advance), initial, stacked)
    return swept_back[1].reshape(total, value_rows.shape[1])

def reference(projected, out_grads, conv_weight, doc_lengths):
    total = projected.shape[0]
    positions = jnp.arange(total, dtype=jnp.int32)
    starts = (jnp.cumsum(doc_lengths) - doc_lengths).astype(jnp.int32)
    begins = lax.optimization_barrier(jnp.max(jnp.where(starts[None, :] <= positions[:, None], starts[None, :], 0), axis=1)).astype(jnp.int32)
    offsets = positions - begins
    keep_one = (offsets >= 1).astype(jnp.float32)[:, None]
    keep_two = (offsets >= 2).astype(jnp.float32)[:, None]
    head_width = 2 * KEY_DIM + HEAD_DIM
    scale_key = KEY_DIM ** (-0.25)

    def per_head(triple):
        return head_attention(triple, begins)

    def layer(signal, weights):
        mixed_rows = weights[0] * signal + weights[1] * shift_rows(signal, 1) * keep_one + weights[2] * shift_rows(signal, 2) * keep_two
        shaped = jnp.transpose(mixed_rows.reshape(total, HEADS, head_width), (1, 0, 2))
        queries = shaped[:, :, :KEY_DIM] * scale_key
        keys_all = shaped[:, :, KEY_DIM:2 * KEY_DIM] * scale_key
        values_all = shaped[:, :, 2 * KEY_DIM:]
        attended = lax.map(per_head, (queries, keys_all, values_all))
        return jnp.transpose(attended, (1, 0, 2)).reshape(total, HEADS * HEAD_DIM)
    primal, pullback = jax.vjp(layer, projected, conv_weight)
    results = pullback(out_grads)
    return (results[0], results[1])
```

```python
import math

import jax
import jax.numpy as jnp
import numpy as np
from jax import lax
from jax.sharding import PartitionSpec as P

KEY_DIM = 16
HEAD_DIM = 128


HIGHEST = lax.Precision.HIGHEST


def segment_sum(gathered, flags, here, reverse):
    count = gathered.shape[0]
    index = jnp.arange(count, dtype=jnp.int32)
    started = flags > 0.5
    if reverse:
        bound = jnp.min(jnp.where((index > here) & started, index, count - 1))
        take = (index > here) & (index <= bound)
    else:
        bound = jnp.max(jnp.where((index < here) & started, index, 0))
        take = (index >= bound) & (index < here)
    return jnp.sum(jnp.where(take[:, None], gathered, 0.0), axis=0)


def carried_in(state, norm, extra, flags, axis, reverse):
    here = lax.axis_index(axis)
    size = state.size
    packed = jnp.concatenate([state.reshape(-1), norm.reshape(-1), extra])
    width = 128
    padded = jnp.pad(packed, (0, -packed.shape[0] % width)).reshape(-1, width)
    gathered = lax.all_gather(padded, axis).reshape(lax.axis_size(axis), -1)
    if flags is None:
        flags = gathered[:, packed.shape[0] - 1]
    total = segment_sum(gathered[:, : size + norm.size], flags, here, reverse)
    return (total[:size].reshape(state.shape), total[size:].reshape(norm.shape), flags)


def passed_along(value, axis, steps):
    count = lax.axis_size(axis)
    initial, last = (max(0, -steps), min(count, count - steps))
    return lax.ppermute(value, axis, [(source, source + steps) for source in range(initial, last)])


def feature_map(columns):
    key_size = columns.shape[1]
    upper_i, upper_j = np.triu_indices(key_size)
    factors = np.where(upper_i == upper_j, 1.0 / math.sqrt(2.0), 1.0).astype(np.float32)
    products = columns[:, upper_i, :] * columns[:, upper_j, :] * jnp.asarray(factors)[None, :, None]
    constant = jnp.ones((columns.shape[0], 1, columns.shape[2]), jnp.float32)
    return jnp.concatenate([constant, columns, products], axis=1)


def doc_place(doc_lengths, anchor, amount):
    positions = anchor + jnp.arange(amount, dtype=jnp.int32)
    starts = jnp.cumsum(doc_lengths) - doc_lengths
    begins = jnp.max(jnp.where(starts[None, :] <= positions[:, None], starts[None, :], 0), axis=1)
    return (begins, positions - begins)


def conv_forward(signal, leading, weights, offsets):
    row_count = signal.shape[0]
    behind = jnp.concatenate([leading, signal], axis=0)
    back_one = behind[1 : row_count + 1] * (offsets[0:row_count] >= 1).astype(jnp.float32)[:, None]
    back_two = behind[0:row_count] * (offsets[0:row_count] >= 2).astype(jnp.float32)[:, None]
    return weights[0] * signal + weights[1] * back_one + weights[2] * back_two


def conv_backward(grad_rows, trailing, signal, leading, weights, offsets):
    row_count = grad_rows.shape[0]
    ahead_rows = jnp.concatenate([grad_rows, trailing], axis=0)
    ahead_one = (
        ahead_rows[1 : row_count + 1]
        * (offsets[1 : row_count + 1] >= 1).astype(jnp.float32)[:, None]
    )
    ahead_two = (
        ahead_rows[2 : row_count + 2]
        * (offsets[2 : row_count + 2] >= 2).astype(jnp.float32)[:, None]
    )
    grad_signal = weights[0] * grad_rows + weights[1] * ahead_one + weights[2] * ahead_two
    behind = jnp.concatenate([leading, signal], axis=0)
    own_one = (offsets[0:row_count] >= 1).astype(jnp.float32)[:, None]
    own_two = (offsets[0:row_count] >= 2).astype(jnp.float32)[:, None]
    grad_weights = jnp.stack(
        [
            jnp.sum(grad_rows * signal, axis=0),
            jnp.sum(grad_rows * behind[1 : row_count + 1] * own_one, axis=0),
            jnp.sum(grad_rows * behind[0:row_count] * own_two, axis=0),
        ],
        axis=0,
    )
    return (grad_signal, grad_weights)


def attention_grads(mixed_rows, out_flat, begins, stretch_start):
    length = mixed_rows.shape[0]
    head_width = 2 * KEY_DIM + HEAD_DIM
    local_heads = mixed_rows.shape[1] // head_width
    block_len = min(128, length)
    blocks = length // block_len
    scale_key = KEY_DIM ** (-0.25)
    shaped = mixed_rows.reshape(length, local_heads, head_width)
    query_cols = jnp.transpose(shaped[:, :, :KEY_DIM], (1, 2, 0)) * scale_key
    key_cols = jnp.transpose(shaped[:, :, KEY_DIM : 2 * KEY_DIM], (1, 2, 0)) * scale_key
    values = shaped[:, :, 2 * KEY_DIM :]
    upstream = out_flat.reshape(length, local_heads, HEAD_DIM)
    query_feat, query_pull = jax.vjp(feature_map, query_cols)
    key_feat, key_pull = jax.vjp(feature_map, key_cols)
    feat_count = query_feat.shape[1]
    last_begin = begins[length - 1]
    has_start = (last_begin >= stretch_start).astype(jnp.float32).reshape(1)
    tail_mask = (begins == last_begin).astype(jnp.float32)
    tail_feat = key_feat * tail_mask[None, None, :]
    tail_state = jnp.einsum("hfl,lhe->hfe", tail_feat, values, precision=HIGHEST)
    tail_norm = jnp.sum(tail_feat, axis=2)
    prefix = carried_in(tail_state, tail_norm, has_start, None, "seq", False)
    flags = prefix[2]
    causal = jnp.arange(block_len)[:, None] >= jnp.arange(block_len)[None, :]
    indices = jnp.arange(blocks, dtype=jnp.int32)

    def forward_block(carried, block_index):
        carry_state, carry_norm = carried
        offset_rows = block_index * block_len
        block_start = stretch_start + offset_rows
        query_blk = lax.dynamic_slice_in_dim(query_feat, offset_rows, block_len, 2)
        key_blk = lax.dynamic_slice_in_dim(key_feat, offset_rows, block_len, 2)
        value_blk = lax.dynamic_slice_in_dim(values, offset_rows, block_len, 0)
        doc_blk = lax.dynamic_slice_in_dim(begins, offset_rows, block_len, 0)
        allowed = causal & (doc_blk[:, None] == doc_blk[None, :])
        scores = jnp.where(
            allowed[None], jnp.einsum("hft,hfs->hts", query_blk, key_blk, precision=HIGHEST), 0.0
        )
        from_carry = (doc_blk < block_start).astype(jnp.float32)
        numerator = jnp.einsum("hts,she->the", scores, value_blk, precision=HIGHEST) + from_carry[
            :, None, None
        ] * jnp.einsum("hft,hfe->the", query_blk, carry_state, precision=HIGHEST)
        denominator = jnp.sum(scores, axis=2) + from_carry[None, :] * jnp.einsum(
            "hft,hf->ht", query_blk, carry_norm, precision=HIGHEST
        )
        block_tail = (doc_blk == doc_blk[block_len - 1]).astype(jnp.float32)
        carry_keep = (doc_blk[block_len - 1] < block_start).astype(jnp.float32)
        tail_keys = key_blk * block_tail[None, None, :]
        next_state = (
            jnp.einsum("hfs,she->hfe", tail_keys, value_blk, precision=HIGHEST)
            + carry_keep * carry_state
        )
        next_norm = jnp.sum(tail_keys, axis=2) + carry_keep * carry_norm
        return ((next_state, next_norm), (numerator, denominator, carry_state, carry_norm, scores))

    forward_out = lax.scan(forward_block, (prefix[0], prefix[1]), indices)
    numerators, denominators, states, norms, kept_scores = forward_out[1]
    denom_rows = jnp.transpose(denominators, (0, 2, 1)).reshape(length, local_heads)
    attended = numerators.reshape(length, local_heads, HEAD_DIM) / denom_rows[:, :, None]
    grad_num = upstream / denom_rows[:, :, None]
    scalar_grad = -jnp.sum(upstream * attended, axis=2) / denom_rows
    lead_mask = (begins < stretch_start).astype(jnp.float32)
    lead_feat = query_feat * lead_mask[None, None, :]
    lead_state = jnp.einsum("hfl,lhe->hfe", lead_feat, grad_num, precision=HIGHEST)
    lead_norm = jnp.einsum("hfl,lh->hf", lead_feat, scalar_grad, precision=HIGHEST)
    suffix = carried_in(lead_state, lead_norm, jnp.zeros((0,), jnp.float32), flags, "seq", True)

    def backward_block(carried, inputs):
        back_state, back_norm = carried
        block_index, carry_state, carry_norm, scores = inputs
        offset_rows = block_index * block_len
        block_start = stretch_start + offset_rows
        query_blk = lax.dynamic_slice_in_dim(query_feat, offset_rows, block_len, 2)
        key_blk = lax.dynamic_slice_in_dim(key_feat, offset_rows, block_len, 2)
        value_blk = lax.dynamic_slice_in_dim(values, offset_rows, block_len, 0)
        doc_blk = lax.dynamic_slice_in_dim(begins, offset_rows, block_len, 0)
        grad_blk = lax.dynamic_slice_in_dim(grad_num, offset_rows, block_len, 0)
        scalar_blk = lax.dynamic_slice_in_dim(scalar_grad, offset_rows, block_len, 0)
        scalar_cols = scalar_blk.T
        allowed = causal & (doc_blk[:, None] == doc_blk[None, :])
        dscores = jnp.where(
            allowed[None],
            jnp.einsum("the,she->hts", grad_blk, value_blk, precision=HIGHEST)
            + scalar_cols[:, :, None],
            0.0,
        )
        from_carry = (doc_blk < block_start).astype(jnp.float32)
        block_tail = (doc_blk == doc_blk[block_len - 1]).astype(jnp.float32)
        carry_keep = (doc_blk[block_len - 1] < block_start).astype(jnp.float32)
        grad_query = jnp.einsum("hts,hfs->hft", dscores, key_blk, precision=HIGHEST) + from_carry[
            None, None, :
        ] * (
            jnp.einsum("hfe,the->hft", carry_state, grad_blk, precision=HIGHEST)
            + carry_norm[:, :, None] * scalar_cols[:, None, :]
        )
        grad_key = jnp.einsum("hts,hft->hfs", dscores, query_blk, precision=HIGHEST) + block_tail[
            None, None, :
        ] * (
            jnp.einsum("hfe,she->hfs", back_state, value_blk, precision=HIGHEST)
            + back_norm[:, :, None]
        )
        grad_value = jnp.einsum("hts,the->she", scores, grad_blk, precision=HIGHEST) + block_tail[
            :, None, None
        ] * jnp.einsum("hfs,hfe->she", key_blk, back_state, precision=HIGHEST)
        lead_blk = query_blk * from_carry[None, None, :]
        next_state = (
            jnp.einsum("hft,the->hfe", lead_blk, grad_blk, precision=HIGHEST)
            + carry_keep * back_state
        )
        next_norm = (
            jnp.einsum("hft,th->hf", lead_blk, scalar_blk, precision=HIGHEST)
            + carry_keep * back_norm
        )
        return ((next_state, next_norm), (grad_query, grad_key, grad_value))

    swept_back = lax.scan(
        backward_block, (suffix[0], suffix[1]), (indices, states, norms, kept_scores), reverse=True
    )
    grad_qblocks, grad_kblocks, grad_vblocks = swept_back[1]
    query_grad = jnp.transpose(grad_qblocks, (1, 2, 0, 3)).reshape(local_heads, feat_count, length)
    key_grad = jnp.transpose(grad_kblocks, (1, 2, 0, 3)).reshape(local_heads, feat_count, length)
    value_grad = grad_vblocks.reshape(length, local_heads, HEAD_DIM)
    query_in = jnp.transpose(query_pull(query_grad)[0] * scale_key, (2, 0, 1))
    key_in = jnp.transpose(key_pull(key_grad)[0] * scale_key, (2, 0, 1))
    return jnp.concatenate([query_in, key_in, value_grad], axis=2).reshape(
        length, local_heads * head_width
    )


def on_device(projected, out_grads, conv_weight, doc_lengths):
    row_count = projected.shape[0]
    head_count = lax.axis_size("head")
    seq_index = lax.axis_index("seq")
    head_index = lax.axis_index("head")
    group_len = row_count * head_count
    token_base = (seq_index * head_count + head_index) * row_count
    stretch_start = seq_index * group_len
    token_begins, token_offsets = doc_place(doc_lengths, token_base, row_count + 2)
    leading = passed_along(projected[row_count - 2 :], ("seq", "head"), 1)
    outgoing = conv_forward(projected, leading, conv_weight, token_offsets)
    arrived, upstream = (
        lax.all_to_all(outgoing, "head", split_axis=1, concat_axis=0, tiled=True),
        lax.all_to_all(out_grads, "head", split_axis=1, concat_axis=0, tiled=True),
    )
    group_begins, group_offsets = doc_place(doc_lengths, stretch_start, group_len + 2)
    grad_mixed = attention_grads(arrived, upstream, group_begins[:group_len], stretch_start)
    returned = lax.all_to_all(grad_mixed, "head", split_axis=0, concat_axis=1, tiled=True)
    trailing = passed_along(returned[:2], ("seq", "head"), -1)
    grad_projected, weight_part = conv_backward(
        returned, trailing, projected, leading, conv_weight, token_offsets
    )
    grad_conv = lax.psum(weight_part, ("seq", "head"))
    return (grad_projected, grad_conv)


def solution(mesh):
    return jax.shard_map(
        on_device,
        mesh=mesh,
        in_specs=(P(("seq", "head"), None), P(("seq", "head"), None), P(), P()),
        out_specs=(P(("seq", "head"), None), P()),
        check_vma=False,
    )
```

```python
import math

import jax
import jax.numpy as jnp
import numpy as np
from jax import lax
from jax.sharding import PartitionSpec as P

KEY_DIM = 16
HEAD_DIM = 128


HIGHEST = lax.Precision.HIGHEST


def segment_sum(gathered, flags, here, reverse):
    count = gathered.shape[0]
    index = jnp.arange(count, dtype=jnp.int32)
    started = flags > 0.5
    if reverse:
        bound = jnp.min(jnp.where((index > here) & started, index, count - 1))
        take = (index > here) & (index <= bound)
    else:
        bound = jnp.max(jnp.where((index < here) & started, index, 0))
        take = (index >= bound) & (index < here)
    return jnp.sum(jnp.where(take[:, None], gathered, 0.0), axis=0)


def carried_in(state, norm, extra, flags, axis, reverse):
    here = lax.axis_index(axis)
    size = state.size
    packed = jnp.concatenate([state.reshape(-1), norm.reshape(-1), extra])
    width = 128
    padded = jnp.pad(packed, (0, -packed.shape[0] % width)).reshape(-1, width)
    gathered = lax.all_gather(padded, axis).reshape(lax.axis_size(axis), -1)
    if flags is None:
        flags = gathered[:, packed.shape[0] - 1]
    total = segment_sum(gathered[:, : size + norm.size], flags, here, reverse)
    return (total[:size].reshape(state.shape), total[size:].reshape(norm.shape), flags)


def passed_along(value, axis, steps):
    count = lax.axis_size(axis)
    initial, last = (max(0, -steps), min(count, count - steps))
    return lax.ppermute(value, axis, [(source, source + steps) for source in range(initial, last)])


def feature_map(columns):
    key_size = columns.shape[1]
    upper_i, upper_j = np.triu_indices(key_size)
    factors = np.where(upper_i == upper_j, 1.0 / math.sqrt(2.0), 1.0).astype(np.float32)
    products = columns[:, upper_i, :] * columns[:, upper_j, :] * jnp.asarray(factors)[None, :, None]
    constant = jnp.ones((columns.shape[0], 1, columns.shape[2]), jnp.float32)
    return jnp.concatenate([constant, columns, products], axis=1)


def doc_place(doc_lengths, anchor, amount):
    positions = anchor + jnp.arange(amount, dtype=jnp.int32)
    starts = jnp.cumsum(doc_lengths) - doc_lengths
    begins = jnp.max(jnp.where(starts[None, :] <= positions[:, None], starts[None, :], 0), axis=1)
    return (begins, positions - begins)


def conv_forward(signal, leading, weights, offsets):
    row_count = signal.shape[0]
    behind = jnp.concatenate([leading, signal], axis=0)
    back_one = behind[1 : row_count + 1] * (offsets[0:row_count] >= 1).astype(jnp.float32)[:, None]
    back_two = behind[0:row_count] * (offsets[0:row_count] >= 2).astype(jnp.float32)[:, None]
    return weights[0] * signal + weights[1] * back_one + weights[2] * back_two


def conv_backward(grad_rows, trailing, signal, leading, weights, offsets):
    row_count = grad_rows.shape[0]
    ahead_rows = jnp.concatenate([grad_rows, trailing], axis=0)
    ahead_one = (
        ahead_rows[1 : row_count + 1]
        * (offsets[1 : row_count + 1] >= 1).astype(jnp.float32)[:, None]
    )
    ahead_two = (
        ahead_rows[2 : row_count + 2]
        * (offsets[2 : row_count + 2] >= 2).astype(jnp.float32)[:, None]
    )
    grad_signal = weights[0] * grad_rows + weights[1] * ahead_one + weights[2] * ahead_two
    behind = jnp.concatenate([leading, signal], axis=0)
    own_one = (offsets[0:row_count] >= 1).astype(jnp.float32)[:, None]
    own_two = (offsets[0:row_count] >= 2).astype(jnp.float32)[:, None]
    grad_weights = jnp.stack(
        [
            jnp.sum(grad_rows * signal, axis=0),
            jnp.sum(grad_rows * behind[1 : row_count + 1] * own_one, axis=0),
            jnp.sum(grad_rows * behind[0:row_count] * own_two, axis=0),
        ],
        axis=0,
    )
    return (grad_signal, grad_weights)


def attention_grads(mixed_rows, out_flat, begins, stretch_start):
    length = mixed_rows.shape[0]
    head_width = 2 * KEY_DIM + HEAD_DIM
    local_heads = mixed_rows.shape[1] // head_width
    block_len = min(128, length)
    blocks = length // block_len
    scale_key = KEY_DIM ** (-0.25)
    shaped = mixed_rows.reshape(length, local_heads, head_width)
    query_cols = jnp.transpose(shaped[:, :, :KEY_DIM], (1, 2, 0)) * scale_key
    key_cols = jnp.transpose(shaped[:, :, KEY_DIM : 2 * KEY_DIM], (1, 2, 0)) * scale_key
    values = shaped[:, :, 2 * KEY_DIM :]
    upstream = out_flat.reshape(length, local_heads, HEAD_DIM)
    query_feat, query_pull = jax.vjp(feature_map, query_cols)
    key_feat, key_pull = jax.vjp(feature_map, key_cols)
    feat_count = query_feat.shape[1]
    last_begin = begins[length - 1]
    has_start = (last_begin >= stretch_start).astype(jnp.float32).reshape(1)
    tail_mask = (begins == last_begin).astype(jnp.float32)
    tail_feat = key_feat * tail_mask[None, None, :]
    tail_state = jnp.einsum("hfl,lhe->hfe", tail_feat, values, precision=HIGHEST)
    tail_norm = jnp.sum(tail_feat, axis=2)
    prefix = carried_in(tail_state, tail_norm, has_start, None, "seq", False)
    flags = prefix[2]
    causal = jnp.arange(block_len)[:, None] >= jnp.arange(block_len)[None, :]
    query_blk = jnp.transpose(query_feat.reshape(local_heads, feat_count, blocks, block_len), (2, 0, 1, 3))
    key_blk = jnp.transpose(key_feat.reshape(local_heads, feat_count, blocks, block_len), (2, 0, 1, 3))
    value_blk = values.reshape(blocks, block_len, local_heads, HEAD_DIM)
    doc_blk = begins.reshape(blocks, block_len)
    block_start = stretch_start + jnp.arange(blocks, dtype=jnp.int32) * block_len
    allowed = causal[None] & (doc_blk[:, :, None] == doc_blk[:, None, :])
    from_carry = (doc_blk < block_start[:, None]).astype(jnp.float32)
    block_tail = (doc_blk == doc_blk[:, block_len - 1 :]).astype(jnp.float32)
    breaks = (doc_blk[:, block_len - 1] >= block_start).astype(jnp.int32)
    upto = jnp.cumsum(breaks)
    before = upto - breaks
    order = jnp.arange(blocks)
    ahead_w = ((order[None, :] < order[:, None]) & (before[:, None] == upto[None, :])).astype(jnp.float32)
    ahead_p = (before == 0).astype(jnp.float32)
    behind_w = ((order[None, :] > order[:, None]) & (before[None, :] == upto[:, None])).astype(jnp.float32)
    behind_p = (upto[blocks - 1] == upto).astype(jnp.float32)
    scores = jnp.where(
        allowed[:, None], jnp.einsum("bhft,bhfs->bhts", query_blk, key_blk, precision=HIGHEST), 0.0
    )
    tail_keys = key_blk * block_tail[:, None, None, :]
    tail_states = jnp.einsum("bhfs,bshe->bhfe", tail_keys, value_blk, precision=HIGHEST)
    tail_norms = jnp.sum(tail_keys, axis=3)
    carry_state = jnp.einsum("bc,chfe->bhfe", ahead_w, tail_states, precision=HIGHEST) + ahead_p[
        :, None, None, None
    ] * prefix[0][None]
    carry_norm = jnp.einsum("bc,chf->bhf", ahead_w, tail_norms, precision=HIGHEST) + ahead_p[
        :, None, None
    ] * prefix[1][None]
    numerators = jnp.einsum("bhts,bshe->bthe", scores, value_blk, precision=HIGHEST) + from_carry[
        :, :, None, None
    ] * jnp.einsum("bhft,bhfe->bthe", query_blk, carry_state, precision=HIGHEST)
    denominators = jnp.sum(scores, axis=3) + from_carry[:, None, :] * jnp.einsum(
        "bhft,bhf->bht", query_blk, carry_norm, precision=HIGHEST
    )
    denom_rows = jnp.transpose(denominators, (0, 2, 1)).reshape(length, local_heads)
    attended = numerators.reshape(length, local_heads, HEAD_DIM) / denom_rows[:, :, None]
    grad_num = upstream / denom_rows[:, :, None]
    scalar_grad = -jnp.sum(upstream * attended, axis=2) / denom_rows
    lead_mask = (begins < stretch_start).astype(jnp.float32)
    lead_feat = query_feat * lead_mask[None, None, :]
    lead_state = jnp.einsum("hfl,lhe->hfe", lead_feat, grad_num, precision=HIGHEST)
    lead_norm = jnp.einsum("hfl,lh->hf", lead_feat, scalar_grad, precision=HIGHEST)
    suffix = carried_in(lead_state, lead_norm, jnp.zeros((0,), jnp.float32), flags, "seq", True)
    grad_blk = grad_num.reshape(blocks, block_len, local_heads, HEAD_DIM)
    scalar_cols = jnp.transpose(scalar_grad.reshape(blocks, block_len, local_heads), (0, 2, 1))
    dscores = jnp.where(
        allowed[:, None],
        jnp.einsum("bthe,bshe->bhts", grad_blk, value_blk, precision=HIGHEST)
        + scalar_cols[:, :, :, None],
        0.0,
    )
    lead_blk = query_blk * from_carry[:, None, None, :]
    lead_states = jnp.einsum("bhft,bthe->bhfe", lead_blk, grad_blk, precision=HIGHEST)
    lead_norms = jnp.einsum("bhft,bht->bhf", lead_blk, scalar_cols, precision=HIGHEST)
    back_state = jnp.einsum("bc,chfe->bhfe", behind_w, lead_states, precision=HIGHEST) + behind_p[
        :, None, None, None
    ] * suffix[0][None]
    back_norm = jnp.einsum("bc,chf->bhf", behind_w, lead_norms, precision=HIGHEST) + behind_p[
        :, None, None
    ] * suffix[1][None]
    grad_qblocks = jnp.einsum("bhts,bhfs->bhft", dscores, key_blk, precision=HIGHEST) + from_carry[
        :, None, None, :
    ] * (
        jnp.einsum("bhfe,bthe->bhft", carry_state, grad_blk, precision=HIGHEST)
        + carry_norm[:, :, :, None] * scalar_cols[:, :, None, :]
    )
    grad_kblocks = jnp.einsum("bhts,bhft->bhfs", dscores, query_blk, precision=HIGHEST) + block_tail[
        :, None, None, :
    ] * (
        jnp.einsum("bhfe,bshe->bhfs", back_state, value_blk, precision=HIGHEST)
        + back_norm[:, :, :, None]
    )
    grad_vblocks = jnp.einsum("bhts,bthe->bshe", scores, grad_blk, precision=HIGHEST) + block_tail[
        :, :, None, None
    ] * jnp.einsum("bhfs,bhfe->bshe", key_blk, back_state, precision=HIGHEST)
    query_grad = jnp.transpose(grad_qblocks, (1, 2, 0, 3)).reshape(local_heads, feat_count, length)
    key_grad = jnp.transpose(grad_kblocks, (1, 2, 0, 3)).reshape(local_heads, feat_count, length)
    value_grad = grad_vblocks.reshape(length, local_heads, HEAD_DIM)
    query_in = jnp.transpose(query_pull(query_grad)[0] * scale_key, (2, 0, 1))
    key_in = jnp.transpose(key_pull(key_grad)[0] * scale_key, (2, 0, 1))
    return jnp.concatenate([query_in, key_in, value_grad], axis=2).reshape(
        length, local_heads * head_width
    )


def on_device(projected, out_grads, conv_weight, doc_lengths):
    row_count = projected.shape[0]
    head_count = lax.axis_size("head")
    seq_index = lax.axis_index("seq")
    head_index = lax.axis_index("head")
    group_len = row_count * head_count
    token_base = (seq_index * head_count + head_index) * row_count
    stretch_start = seq_index * group_len
    token_begins, token_offsets = doc_place(doc_lengths, token_base, row_count + 2)
    leading = passed_along(projected[row_count - 2 :], ("seq", "head"), 1)
    outgoing = conv_forward(projected, leading, conv_weight, token_offsets)
    arrived, upstream = (
        lax.all_to_all(outgoing, "head", split_axis=1, concat_axis=0, tiled=True),
        lax.all_to_all(out_grads, "head", split_axis=1, concat_axis=0, tiled=True),
    )
    group_begins, group_offsets = doc_place(doc_lengths, stretch_start, group_len + 2)
    grad_mixed = attention_grads(arrived, upstream, group_begins[:group_len], stretch_start)
    returned = lax.all_to_all(grad_mixed, "head", split_axis=0, concat_axis=1, tiled=True)
    trailing = passed_along(returned[:2], ("seq", "head"), -1)
    grad_projected, weight_part = conv_backward(
        returned, trailing, projected, leading, conv_weight, token_offsets
    )
    grad_conv = lax.psum(weight_part, ("seq", "head"))
    return (grad_projected, grad_conv)


def solution(mesh):
    return jax.shard_map(
        on_device,
        mesh=mesh,
        in_specs=(P(("seq", "head"), None), P(("seq", "head"), None), P(), P()),
        out_specs=(P(("seq", "head"), None), P()),
        check_vma=False,
    )
```

```python
import math

import jax
import jax.numpy as jnp
import numpy as np
from jax import lax
from jax.sharding import PartitionSpec as P

KEY_DIM = 16
HEAD_DIM = 128


HIGHEST = lax.Precision.HIGHEST


def segment_sum(gathered, flags, here, reverse):
    count = gathered.shape[0]
    index = jnp.arange(count, dtype=jnp.int32)
    started = flags > 0.5
    if reverse:
        bound = jnp.min(jnp.where((index > here) & started, index, count - 1))
        take = (index > here) & (index <= bound)
    else:
        bound = jnp.max(jnp.where((index < here) & started, index, 0))
        take = (index >= bound) & (index < here)
    return jnp.sum(jnp.where(take[:, None], gathered, 0.0), axis=0)


def carried_in(state, norm, extra, flags, axis, reverse):
    here = lax.axis_index(axis)
    size = state.size
    packed = jnp.concatenate([state.reshape(-1), norm.reshape(-1), extra])
    width = 128
    padded = jnp.pad(packed, (0, -packed.shape[0] % width)).reshape(-1, width)
    gathered = lax.all_gather(padded, axis).reshape(lax.axis_size(axis), -1)
    if flags is None:
        flags = gathered[:, packed.shape[0] - 1]
    total = segment_sum(gathered[:, : size + norm.size], flags, here, reverse)
    return (total[:size].reshape(state.shape), total[size:].reshape(norm.shape), flags)


def passed_along(value, axis, steps):
    count = lax.axis_size(axis)
    initial, last = (max(0, -steps), min(count, count - steps))
    return lax.ppermute(value, axis, [(source, source + steps) for source in range(initial, last)])


def feature_map(columns):
    key_size = columns.shape[1]
    upper_i, upper_j = np.triu_indices(key_size)
    factors = np.where(upper_i == upper_j, 1.0 / math.sqrt(2.0), 1.0).astype(np.float32)
    products = columns[:, upper_i, :] * columns[:, upper_j, :] * jnp.asarray(factors)[None, :, None]
    constant = jnp.ones((columns.shape[0], 1, columns.shape[2]), jnp.float32)
    return jnp.concatenate([constant, columns, products], axis=1)


def doc_place(doc_lengths, anchor, amount):
    positions = anchor + jnp.arange(amount, dtype=jnp.int32)
    starts = jnp.cumsum(doc_lengths) - doc_lengths
    begins = jnp.max(jnp.where(starts[None, :] <= positions[:, None], starts[None, :], 0), axis=1)
    return (begins, positions - begins)


def conv_forward(signal, leading, weights, offsets):
    row_count = signal.shape[0]
    behind = jnp.concatenate([leading, signal], axis=0)
    back_one = behind[1 : row_count + 1] * (offsets[0:row_count] >= 1).astype(jnp.float32)[:, None]
    back_two = behind[0:row_count] * (offsets[0:row_count] >= 2).astype(jnp.float32)[:, None]
    return weights[0] * signal + weights[1] * back_one + weights[2] * back_two


def conv_backward(grad_rows, trailing, signal, leading, weights, offsets):
    row_count = grad_rows.shape[0]
    ahead_rows = jnp.concatenate([grad_rows, trailing], axis=0)
    ahead_one = (
        ahead_rows[1 : row_count + 1]
        * (offsets[1 : row_count + 1] >= 1).astype(jnp.float32)[:, None]
    )
    ahead_two = (
        ahead_rows[2 : row_count + 2]
        * (offsets[2 : row_count + 2] >= 2).astype(jnp.float32)[:, None]
    )
    grad_signal = weights[0] * grad_rows + weights[1] * ahead_one + weights[2] * ahead_two
    behind = jnp.concatenate([leading, signal], axis=0)
    own_one = (offsets[0:row_count] >= 1).astype(jnp.float32)[:, None]
    own_two = (offsets[0:row_count] >= 2).astype(jnp.float32)[:, None]
    grad_weights = jnp.stack(
        [
            jnp.sum(grad_rows * signal, axis=0),
            jnp.sum(grad_rows * behind[1 : row_count + 1] * own_one, axis=0),
            jnp.sum(grad_rows * behind[0:row_count] * own_two, axis=0),
        ],
        axis=0,
    )
    return (grad_signal, grad_weights)


def attention_grads(mixed_rows, out_flat, begins, stretch_start):
    length = mixed_rows.shape[0]
    head_width = 2 * KEY_DIM + HEAD_DIM
    local_heads = mixed_rows.shape[1] // head_width
    block_len = min(128, length)
    blocks = length // block_len
    scale_key = KEY_DIM ** (-0.25)
    shaped = mixed_rows.reshape(length, local_heads, head_width)
    query_cols = jnp.transpose(shaped[:, :, :KEY_DIM], (1, 2, 0)) * scale_key
    key_cols = jnp.transpose(shaped[:, :, KEY_DIM : 2 * KEY_DIM], (1, 2, 0)) * scale_key
    values = shaped[:, :, 2 * KEY_DIM :]
    upstream = out_flat.reshape(length, local_heads, HEAD_DIM)
    query_feat, query_pull = jax.vjp(feature_map, query_cols)
    key_feat, key_pull = jax.vjp(feature_map, key_cols)
    feat_count = query_feat.shape[1]
    last_begin = begins[length - 1]
    has_start = (last_begin >= stretch_start).astype(jnp.float32).reshape(1)
    tail_mask = (begins == last_begin).astype(jnp.float32)
    tail_feat = key_feat * tail_mask[None, None, :]
    tail_state = jnp.einsum("hfl,lhe->hfe", tail_feat, values, precision=HIGHEST)
    tail_norm = jnp.sum(tail_feat, axis=2)
    prefix = carried_in(tail_state, tail_norm, has_start, None, "seq", False)
    flags = prefix[2]
    causal = jnp.arange(block_len)[:, None] >= jnp.arange(block_len)[None, :]
    query_blk = jnp.transpose(query_feat.reshape(local_heads, feat_count, blocks, block_len), (2, 0, 1, 3))
    key_blk = jnp.transpose(key_feat.reshape(local_heads, feat_count, blocks, block_len), (2, 0, 1, 3))
    value_blk = values.reshape(blocks, block_len, local_heads, HEAD_DIM)
    doc_blk = begins.reshape(blocks, block_len)
    block_start = stretch_start + jnp.arange(blocks, dtype=jnp.int32) * block_len
    allowed = causal[None] & (doc_blk[:, :, None] == doc_blk[:, None, :])
    from_carry = (doc_blk < block_start[:, None]).astype(jnp.float32)
    block_tail = (doc_blk == doc_blk[:, block_len - 1 :]).astype(jnp.float32)
    breaks = (doc_blk[:, block_len - 1] >= block_start).astype(jnp.int32)
    upto = jnp.cumsum(breaks)
    before = upto - breaks
    order = jnp.arange(blocks)
    ahead_w = ((order[None, :] < order[:, None]) & (before[:, None] == upto[None, :])).astype(jnp.float32)
    ahead_p = (before == 0).astype(jnp.float32)
    behind_w = ((order[None, :] > order[:, None]) & (before[None, :] == upto[:, None])).astype(jnp.float32)
    behind_p = (upto[blocks - 1] == upto).astype(jnp.float32)
    scores = jnp.where(
        allowed[:, None], jnp.einsum("bhft,bhfs->bhts", query_blk, key_blk, precision=HIGHEST), 0.0
    )
    tail_keys = key_blk * block_tail[:, None, None, :]
    tail_states = jnp.einsum("bhfs,bshe->bhfe", tail_keys, value_blk, precision=HIGHEST)
    tail_norms = jnp.sum(tail_keys, axis=3)
    carry_state = jnp.einsum("bc,chfe->bhfe", ahead_w, tail_states, precision=HIGHEST) + ahead_p[
        :, None, None, None
    ] * prefix[0][None]
    carry_norm = jnp.einsum("bc,chf->bhf", ahead_w, tail_norms, precision=HIGHEST) + ahead_p[
        :, None, None
    ] * prefix[1][None]
    numerators = jnp.einsum("bhts,bshe->bthe", scores, value_blk, precision=HIGHEST) + from_carry[
        :, :, None, None
    ] * jnp.einsum("bhft,bhfe->bthe", query_blk, carry_state, precision=HIGHEST)
    denominators = jnp.sum(scores, axis=3) + from_carry[:, None, :] * jnp.einsum(
        "bhft,bhf->bht", query_blk, carry_norm, precision=HIGHEST
    )
    denom_rows = jnp.transpose(denominators, (0, 2, 1)).reshape(length, local_heads)
    attended = numerators.reshape(length, local_heads, HEAD_DIM) / denom_rows[:, :, None]
    grad_num = upstream / denom_rows[:, :, None]
    scalar_grad = -jnp.sum(upstream * attended, axis=2) / denom_rows
    lead_mask = (begins < stretch_start).astype(jnp.float32)
    lead_feat = query_feat * lead_mask[None, None, :]
    lead_state = jnp.einsum("hfl,lhe->hfe", lead_feat, grad_num, precision=HIGHEST)
    lead_norm = jnp.einsum("hfl,lh->hf", lead_feat, scalar_grad, precision=HIGHEST)
    suffix = carried_in(lead_state, lead_norm, jnp.zeros((0,), jnp.float32), flags, "seq", True)
    grad_blk = grad_num.reshape(blocks, block_len, local_heads, HEAD_DIM)
    scalar_cols = jnp.transpose(scalar_grad.reshape(blocks, block_len, local_heads), (0, 2, 1))
    dscores = jnp.where(
        allowed[:, None],
        jnp.einsum("bthe,bshe->bhts", grad_blk, value_blk, precision=HIGHEST)
        + scalar_cols[:, :, :, None],
        0.0,
    )
    lead_blk = query_blk * from_carry[:, None, None, :]
    lead_states = jnp.einsum("bhft,bthe->bhfe", lead_blk, grad_blk, precision=HIGHEST)
    lead_norms = jnp.einsum("bhft,bht->bhf", lead_blk, scalar_cols, precision=HIGHEST)
    back_state = jnp.einsum("bc,chfe->bhfe", behind_w, lead_states, precision=HIGHEST) + behind_p[
        :, None, None, None
    ] * suffix[0][None]
    back_norm = jnp.einsum("bc,chf->bhf", behind_w, lead_norms, precision=HIGHEST) + behind_p[
        :, None, None
    ] * suffix[1][None]
    grad_qblocks = jnp.einsum("bhts,bhfs->bhft", dscores, key_blk, precision=HIGHEST) + from_carry[
        :, None, None, :
    ] * (
        jnp.einsum("bhfe,bthe->bhft", carry_state, grad_blk, precision=HIGHEST)
        + carry_norm[:, :, :, None] * scalar_cols[:, :, None, :]
    )
    grad_kblocks = jnp.einsum("bhts,bhft->bhfs", dscores, query_blk, precision=HIGHEST) + block_tail[
        :, None, None, :
    ] * (
        jnp.einsum("bhfe,bshe->bhfs", back_state, value_blk, precision=HIGHEST)
        + back_norm[:, :, :, None]
    )
    grad_vblocks = jnp.einsum("bhts,bthe->bshe", scores, grad_blk, precision=HIGHEST) + block_tail[
        :, :, None, None
    ] * jnp.einsum("bhfs,bhfe->bshe", key_blk, back_state, precision=HIGHEST)
    query_grad = jnp.transpose(grad_qblocks, (1, 2, 0, 3)).reshape(local_heads, feat_count, length)
    key_grad = jnp.transpose(grad_kblocks, (1, 2, 0, 3)).reshape(local_heads, feat_count, length)
    value_grad = grad_vblocks.reshape(length, local_heads, HEAD_DIM)
    query_in = jnp.transpose(query_pull(query_grad)[0] * scale_key, (2, 0, 1))
    key_in = jnp.transpose(key_pull(key_grad)[0] * scale_key, (2, 0, 1))
    return jnp.concatenate([query_in, key_in, value_grad], axis=2).reshape(
        length, local_heads * head_width
    )


def summed_everywhere(part):
    head_count = lax.axis_size("head")
    mine = lax.psum_scatter(part, "head", scatter_dimension=1, tiled=True)
    total = jnp.sum(lax.all_gather(mine, "seq"), axis=0)
    return lax.all_gather(total, "head", axis=1, tiled=True)


def on_device(projected, out_grads, conv_weight, doc_lengths):
    row_count = projected.shape[0]
    head_count = lax.axis_size("head")
    seq_index = lax.axis_index("seq")
    head_index = lax.axis_index("head")
    group_len = row_count * head_count
    token_base = (seq_index * head_count + head_index) * row_count
    stretch_start = seq_index * group_len
    token_begins, token_offsets = doc_place(doc_lengths, token_base, row_count + 2)
    leading = passed_along(projected[row_count - 2 :], ("seq", "head"), 1)
    outgoing = conv_forward(projected, leading, conv_weight, token_offsets)
    arrived, upstream = (
        lax.all_to_all(outgoing, "head", split_axis=1, concat_axis=0, tiled=True),
        lax.all_to_all(out_grads, "head", split_axis=1, concat_axis=0, tiled=True),
    )
    group_begins, group_offsets = doc_place(doc_lengths, stretch_start, group_len + 2)
    grad_mixed = attention_grads(arrived, upstream, group_begins[:group_len], stretch_start)
    returned = lax.all_to_all(grad_mixed, "head", split_axis=0, concat_axis=1, tiled=True)
    trailing = passed_along(returned[:2], ("seq", "head"), -1)
    grad_projected, weight_part = conv_backward(
        returned, trailing, projected, leading, conv_weight, token_offsets
    )
    grad_conv = summed_everywhere(weight_part)
    return (grad_projected, grad_conv)


def solution(mesh):
    return jax.shard_map(
        on_device,
        mesh=mesh,
        in_specs=(P(("seq", "head"), None), P(("seq", "head"), None), P(), P()),
        out_specs=(P(("seq", "head"), None), P()),
        check_vma=False,
    )
```

```python
import math

import jax
import jax.numpy as jnp
import numpy as np
from jax import lax
from jax.sharding import PartitionSpec as P

KEY_DIM = 16
HEAD_DIM = 128


HIGHEST = lax.Precision.HIGHEST


def segment_sum(gathered, flags, here, reverse):
    count = gathered.shape[0]
    index = jnp.arange(count, dtype=jnp.int32)
    started = flags > 0.5
    if reverse:
        bound = jnp.min(jnp.where((index > here) & started, index, count - 1))
        take = (index > here) & (index <= bound)
    else:
        bound = jnp.max(jnp.where((index < here) & started, index, 0))
        take = (index >= bound) & (index < here)
    return jnp.sum(jnp.where(take[:, None], gathered, 0.0), axis=0)


def carried_in(state, norm, extra, flags, axis, reverse):
    here = lax.axis_index(axis)
    size = state.size
    packed = jnp.concatenate([state.reshape(-1), norm.reshape(-1), extra])
    width = 128
    padded = jnp.pad(packed, (0, -packed.shape[0] % width)).reshape(-1, width)
    gathered = lax.all_gather(padded, axis).reshape(lax.axis_size(axis), -1)
    if flags is None:
        flags = gathered[:, packed.shape[0] - 1]
    total = segment_sum(gathered[:, : size + norm.size], flags, here, reverse)
    return (total[:size].reshape(state.shape), total[size:].reshape(norm.shape), flags)


def passed_along(value, axis, steps):
    count = lax.axis_size(axis)
    initial, last = (max(0, -steps), min(count, count - steps))
    return lax.ppermute(value, axis, [(source, source + steps) for source in range(initial, last)])


def pair_pickers(key_size):
    upper_i, upper_j = np.triu_indices(key_size)
    factors = np.where(upper_i == upper_j, 1.0 / math.sqrt(2.0), 1.0).astype(np.float32)
    eye = np.eye(key_size, dtype=np.float32)
    return (jnp.asarray(eye[upper_i]), jnp.asarray(eye[upper_j]), jnp.asarray(factors))


def feature_map(columns):
    pick_i, pick_j, factors = pair_pickers(columns.shape[1])
    first = jnp.einsum("pk,hkl->hpl", pick_i, columns, precision=HIGHEST)
    second = jnp.einsum("pk,hkl->hpl", pick_j, columns, precision=HIGHEST)
    products = first * second * factors[None, :, None]
    constant = jnp.ones((columns.shape[0], 1, columns.shape[2]), jnp.float32)
    return (jnp.concatenate([constant, columns, products], axis=1), (first, second))


def feature_pull(parts, grad):
    first, second = parts
    key_size = KEY_DIM
    pick_i, pick_j, factors = pair_pickers(key_size)
    pair_grad = grad[:, 1 + key_size :] * factors[None, :, None]
    return (
        grad[:, 1 : 1 + key_size]
        + jnp.einsum("pk,hpl->hkl", pick_i, pair_grad * second, precision=HIGHEST)
        + jnp.einsum("pk,hpl->hkl", pick_j, pair_grad * first, precision=HIGHEST)
    )


def doc_place(doc_lengths, anchor, amount):
    positions = anchor + jnp.arange(amount, dtype=jnp.int32)
    starts = jnp.cumsum(doc_lengths) - doc_lengths
    begins = jnp.max(jnp.where(starts[None, :] <= positions[:, None], starts[None, :], 0), axis=1)
    return (begins, positions - begins)


def conv_forward(signal, leading, weights, offsets):
    row_count = signal.shape[0]
    behind = jnp.concatenate([leading, signal], axis=0)
    back_one = behind[1 : row_count + 1] * (offsets[0:row_count] >= 1).astype(jnp.float32)[:, None]
    back_two = behind[0:row_count] * (offsets[0:row_count] >= 2).astype(jnp.float32)[:, None]
    return weights[0] * signal + weights[1] * back_one + weights[2] * back_two


def conv_backward(grad_rows, trailing, signal, leading, weights, offsets):
    row_count = grad_rows.shape[0]
    ahead_rows = jnp.concatenate([grad_rows, trailing], axis=0)
    ahead_one = (
        ahead_rows[1 : row_count + 1]
        * (offsets[1 : row_count + 1] >= 1).astype(jnp.float32)[:, None]
    )
    ahead_two = (
        ahead_rows[2 : row_count + 2]
        * (offsets[2 : row_count + 2] >= 2).astype(jnp.float32)[:, None]
    )
    grad_signal = weights[0] * grad_rows + weights[1] * ahead_one + weights[2] * ahead_two
    behind = jnp.concatenate([leading, signal], axis=0)
    own_one = (offsets[0:row_count] >= 1).astype(jnp.float32)[:, None]
    own_two = (offsets[0:row_count] >= 2).astype(jnp.float32)[:, None]
    grad_weights = jnp.stack(
        [
            jnp.sum(grad_rows * signal, axis=0),
            jnp.sum(grad_rows * behind[1 : row_count + 1] * own_one, axis=0),
            jnp.sum(grad_rows * behind[0:row_count] * own_two, axis=0),
        ],
        axis=0,
    )
    return (grad_signal, grad_weights)


def attention_grads(mixed_rows, out_flat, begins, stretch_start):
    length = mixed_rows.shape[0]
    head_width = 2 * KEY_DIM + HEAD_DIM
    local_heads = mixed_rows.shape[1] // head_width
    block_len = min(128, length)
    blocks = length // block_len
    scale_key = KEY_DIM ** (-0.25)
    shaped = mixed_rows.reshape(length, local_heads, head_width)
    query_cols = jnp.transpose(shaped[:, :, :KEY_DIM], (1, 2, 0)) * scale_key
    key_cols = jnp.transpose(shaped[:, :, KEY_DIM : 2 * KEY_DIM], (1, 2, 0)) * scale_key
    values = shaped[:, :, 2 * KEY_DIM :]
    upstream = out_flat.reshape(length, local_heads, HEAD_DIM)
    query_feat, query_parts = feature_map(query_cols)
    key_feat, key_parts = feature_map(key_cols)
    feat_count = query_feat.shape[1]
    last_begin = begins[length - 1]
    has_start = (last_begin >= stretch_start).astype(jnp.float32).reshape(1)
    tail_mask = (begins == last_begin).astype(jnp.float32)
    tail_feat = key_feat * tail_mask[None, None, :]
    tail_state = jnp.einsum("hfl,lhe->hfe", tail_feat, values, precision=HIGHEST)
    tail_norm = jnp.sum(tail_feat, axis=2)
    prefix = carried_in(tail_state, tail_norm, has_start, None, "seq", False)
    flags = prefix[2]
    causal = jnp.arange(block_len)[:, None] >= jnp.arange(block_len)[None, :]
    query_blk = jnp.transpose(query_feat.reshape(local_heads, feat_count, blocks, block_len), (2, 0, 1, 3))
    key_blk = jnp.transpose(key_feat.reshape(local_heads, feat_count, blocks, block_len), (2, 0, 1, 3))
    value_blk = values.reshape(blocks, block_len, local_heads, HEAD_DIM)
    doc_blk = begins.reshape(blocks, block_len)
    block_start = stretch_start + jnp.arange(blocks, dtype=jnp.int32) * block_len
    allowed = causal[None] & (doc_blk[:, :, None] == doc_blk[:, None, :])
    from_carry = (doc_blk < block_start[:, None]).astype(jnp.float32)
    block_tail = (doc_blk == doc_blk[:, block_len - 1 :]).astype(jnp.float32)
    breaks = (doc_blk[:, block_len - 1] >= block_start).astype(jnp.int32)
    upto = jnp.cumsum(breaks)
    before = upto - breaks
    order = jnp.arange(blocks)
    ahead_w = ((order[None, :] < order[:, None]) & (before[:, None] == upto[None, :])).astype(jnp.float32)
    ahead_p = (before == 0).astype(jnp.float32)
    behind_w = ((order[None, :] > order[:, None]) & (before[None, :] == upto[:, None])).astype(jnp.float32)
    behind_p = (upto[blocks - 1] == upto).astype(jnp.float32)
    scores = jnp.where(
        allowed[:, None], jnp.einsum("bhft,bhfs->bhts", query_blk, key_blk, precision=HIGHEST), 0.0
    )
    tail_keys = key_blk * block_tail[:, None, None, :]
    tail_states = jnp.einsum("bhfs,bshe->bhfe", tail_keys, value_blk, precision=HIGHEST)
    tail_norms = jnp.sum(tail_keys, axis=3)
    carry_state = jnp.einsum("bc,chfe->bhfe", ahead_w, tail_states, precision=HIGHEST) + ahead_p[
        :, None, None, None
    ] * prefix[0][None]
    carry_norm = jnp.einsum("bc,chf->bhf", ahead_w, tail_norms, precision=HIGHEST) + ahead_p[
        :, None, None
    ] * prefix[1][None]
    numerators = jnp.einsum("bhts,bshe->bthe", scores, value_blk, precision=HIGHEST) + from_carry[
        :, :, None, None
    ] * jnp.einsum("bhft,bhfe->bthe", query_blk, carry_state, precision=HIGHEST)
    denominators = jnp.sum(scores, axis=3) + from_carry[:, None, :] * jnp.einsum(
        "bhft,bhf->bht", query_blk, carry_norm, precision=HIGHEST
    )
    denom_rows = jnp.transpose(denominators, (0, 2, 1)).reshape(length, local_heads)
    attended = numerators.reshape(length, local_heads, HEAD_DIM) / denom_rows[:, :, None]
    grad_num = upstream / denom_rows[:, :, None]
    scalar_grad = -jnp.sum(upstream * attended, axis=2) / denom_rows
    lead_mask = (begins < stretch_start).astype(jnp.float32)
    lead_feat = query_feat * lead_mask[None, None, :]
    lead_state = jnp.einsum("hfl,lhe->hfe", lead_feat, grad_num, precision=HIGHEST)
    lead_norm = jnp.einsum("hfl,lh->hf", lead_feat, scalar_grad, precision=HIGHEST)
    suffix = carried_in(lead_state, lead_norm, jnp.zeros((0,), jnp.float32), flags, "seq", True)
    grad_blk = grad_num.reshape(blocks, block_len, local_heads, HEAD_DIM)
    scalar_cols = jnp.transpose(scalar_grad.reshape(blocks, block_len, local_heads), (0, 2, 1))
    dscores = jnp.where(
        allowed[:, None],
        jnp.einsum("bthe,bshe->bhts", grad_blk, value_blk, precision=HIGHEST)
        + scalar_cols[:, :, :, None],
        0.0,
    )
    lead_blk = query_blk * from_carry[:, None, None, :]
    lead_states = jnp.einsum("bhft,bthe->bhfe", lead_blk, grad_blk, precision=HIGHEST)
    lead_norms = jnp.einsum("bhft,bht->bhf", lead_blk, scalar_cols, precision=HIGHEST)
    back_state = jnp.einsum("bc,chfe->bhfe", behind_w, lead_states, precision=HIGHEST) + behind_p[
        :, None, None, None
    ] * suffix[0][None]
    back_norm = jnp.einsum("bc,chf->bhf", behind_w, lead_norms, precision=HIGHEST) + behind_p[
        :, None, None
    ] * suffix[1][None]
    grad_qblocks = jnp.einsum("bhts,bhfs->bhft", dscores, key_blk, precision=HIGHEST) + from_carry[
        :, None, None, :
    ] * (
        jnp.einsum("bhfe,bthe->bhft", carry_state, grad_blk, precision=HIGHEST)
        + carry_norm[:, :, :, None] * scalar_cols[:, :, None, :]
    )
    grad_kblocks = jnp.einsum("bhts,bhft->bhfs", dscores, query_blk, precision=HIGHEST) + block_tail[
        :, None, None, :
    ] * (
        jnp.einsum("bhfe,bshe->bhfs", back_state, value_blk, precision=HIGHEST)
        + back_norm[:, :, :, None]
    )
    grad_vblocks = jnp.einsum("bhts,bthe->bshe", scores, grad_blk, precision=HIGHEST) + block_tail[
        :, :, None, None
    ] * jnp.einsum("bhfs,bhfe->bshe", key_blk, back_state, precision=HIGHEST)
    query_grad = jnp.transpose(grad_qblocks, (1, 2, 0, 3)).reshape(local_heads, feat_count, length)
    key_grad = jnp.transpose(grad_kblocks, (1, 2, 0, 3)).reshape(local_heads, feat_count, length)
    value_grad = grad_vblocks.reshape(length, local_heads, HEAD_DIM)
    query_in = jnp.transpose(feature_pull(query_parts, query_grad) * scale_key, (2, 0, 1))
    key_in = jnp.transpose(feature_pull(key_parts, key_grad) * scale_key, (2, 0, 1))
    return jnp.concatenate([query_in, key_in, value_grad], axis=2).reshape(
        length, local_heads * head_width
    )


def on_device(projected, out_grads, conv_weight, doc_lengths):
    row_count = projected.shape[0]
    head_count = lax.axis_size("head")
    seq_index = lax.axis_index("seq")
    head_index = lax.axis_index("head")
    group_len = row_count * head_count
    token_base = (seq_index * head_count + head_index) * row_count
    stretch_start = seq_index * group_len
    token_begins, token_offsets = doc_place(doc_lengths, token_base, row_count + 2)
    leading = passed_along(projected[row_count - 2 :], ("seq", "head"), 1)
    outgoing = conv_forward(projected, leading, conv_weight, token_offsets)
    arrived, upstream = (
        lax.all_to_all(outgoing, "head", split_axis=1, concat_axis=0, tiled=True),
        lax.all_to_all(out_grads, "head", split_axis=1, concat_axis=0, tiled=True),
    )
    group_begins, group_offsets = doc_place(doc_lengths, stretch_start, group_len + 2)
    grad_mixed = attention_grads(arrived, upstream, group_begins[:group_len], stretch_start)
    returned = lax.all_to_all(grad_mixed, "head", split_axis=0, concat_axis=1, tiled=True)
    trailing = passed_along(returned[:2], ("seq", "head"), -1)
    grad_projected, weight_part = conv_backward(
        returned, trailing, projected, leading, conv_weight, token_offsets
    )
    grad_conv = lax.psum(weight_part, ("seq", "head"))
    return (grad_projected, grad_conv)


def solution(mesh):
    return jax.shard_map(
        on_device,
        mesh=mesh,
        in_specs=(P(("seq", "head"), None), P(("seq", "head"), None), P(), P()),
        out_specs=(P(("seq", "head"), None), P()),
        check_vma=False,
    )
```

```python
import math

import jax
import jax.numpy as jnp
import numpy as np
from jax import lax
from jax.sharding import PartitionSpec as P

KEY_DIM = 16
HEAD_DIM = 128


HIGHEST = lax.Precision.HIGHEST
FAST = lax.Precision.HIGH


def segment_sum(gathered, flags, here, reverse):
    count = gathered.shape[0]
    index = jnp.arange(count, dtype=jnp.int32)
    started = flags > 0.5
    if reverse:
        bound = jnp.min(jnp.where((index > here) & started, index, count - 1))
        take = (index > here) & (index <= bound)
    else:
        bound = jnp.max(jnp.where((index < here) & started, index, 0))
        take = (index >= bound) & (index < here)
    return jnp.sum(jnp.where(take[:, None], gathered, 0.0), axis=0)


def carried_in(state, norm, extra, flags, axis, reverse):
    here = lax.axis_index(axis)
    size = state.size
    packed = jnp.concatenate([state.reshape(-1), norm.reshape(-1), extra])
    width = 128
    padded = jnp.pad(packed, (0, -packed.shape[0] % width)).reshape(-1, width)
    gathered = lax.all_gather(padded, axis).reshape(lax.axis_size(axis), -1)
    if flags is None:
        flags = gathered[:, packed.shape[0] - 1]
    total = segment_sum(gathered[:, : size + norm.size], flags, here, reverse)
    return (total[:size].reshape(state.shape), total[size:].reshape(norm.shape), flags)


def passed_along(value, axis, steps):
    count = lax.axis_size(axis)
    initial, last = (max(0, -steps), min(count, count - steps))
    return lax.ppermute(value, axis, [(source, source + steps) for source in range(initial, last)])


def pair_pickers(key_size):
    upper_i, upper_j = np.triu_indices(key_size)
    factors = np.where(upper_i == upper_j, 1.0 / math.sqrt(2.0), 1.0).astype(np.float32)
    eye = np.eye(key_size, dtype=np.float32)
    return (jnp.asarray(eye[upper_i]), jnp.asarray(eye[upper_j]), jnp.asarray(factors))


def feature_map(columns):
    pick_i, pick_j, factors = pair_pickers(columns.shape[1])
    first = jnp.einsum("pk,hkl->hpl", pick_i, columns, precision=HIGHEST)
    second = jnp.einsum("pk,hkl->hpl", pick_j, columns, precision=HIGHEST)
    products = first * second * factors[None, :, None]
    constant = jnp.ones((columns.shape[0], 1, columns.shape[2]), jnp.float32)
    return (jnp.concatenate([constant, columns, products], axis=1), (first, second))


def feature_pull(parts, grad):
    first, second = parts
    key_size = KEY_DIM
    pick_i, pick_j, factors = pair_pickers(key_size)
    pair_grad = grad[:, 1 + key_size :] * factors[None, :, None]
    return (
        grad[:, 1 : 1 + key_size]
        + jnp.einsum("pk,hpl->hkl", pick_i, pair_grad * second, precision=HIGHEST)
        + jnp.einsum("pk,hpl->hkl", pick_j, pair_grad * first, precision=HIGHEST)
    )


def doc_place(doc_lengths, anchor, amount):
    positions = anchor + jnp.arange(amount, dtype=jnp.int32)
    starts = jnp.cumsum(doc_lengths) - doc_lengths
    begins = jnp.max(jnp.where(starts[None, :] <= positions[:, None], starts[None, :], 0), axis=1)
    return (begins, positions - begins)


def conv_forward(signal, leading, weights, offsets):
    row_count = signal.shape[0]
    behind = jnp.concatenate([leading, signal], axis=0)
    back_one = behind[1 : row_count + 1] * (offsets[0:row_count] >= 1).astype(jnp.float32)[:, None]
    back_two = behind[0:row_count] * (offsets[0:row_count] >= 2).astype(jnp.float32)[:, None]
    return weights[0] * signal + weights[1] * back_one + weights[2] * back_two


def conv_backward(grad_rows, trailing, signal, leading, weights, offsets):
    row_count = grad_rows.shape[0]
    ahead_rows = jnp.concatenate([grad_rows, trailing], axis=0)
    ahead_one = (
        ahead_rows[1 : row_count + 1]
        * (offsets[1 : row_count + 1] >= 1).astype(jnp.float32)[:, None]
    )
    ahead_two = (
        ahead_rows[2 : row_count + 2]
        * (offsets[2 : row_count + 2] >= 2).astype(jnp.float32)[:, None]
    )
    grad_signal = weights[0] * grad_rows + weights[1] * ahead_one + weights[2] * ahead_two
    behind = jnp.concatenate([leading, signal], axis=0)
    own_one = (offsets[0:row_count] >= 1).astype(jnp.float32)[:, None]
    own_two = (offsets[0:row_count] >= 2).astype(jnp.float32)[:, None]
    grad_weights = jnp.stack(
        [
            jnp.sum(grad_rows * signal, axis=0),
            jnp.sum(grad_rows * behind[1 : row_count + 1] * own_one, axis=0),
            jnp.sum(grad_rows * behind[0:row_count] * own_two, axis=0),
        ],
        axis=0,
    )
    return (grad_signal, grad_weights)


def attention_grads(mixed_rows, out_flat, begins, stretch_start):
    length = mixed_rows.shape[0]
    head_width = 2 * KEY_DIM + HEAD_DIM
    local_heads = mixed_rows.shape[1] // head_width
    block_len = min(128, length)
    blocks = length // block_len
    scale_key = KEY_DIM ** (-0.25)
    shaped = mixed_rows.reshape(length, local_heads, head_width)
    query_cols = jnp.transpose(shaped[:, :, :KEY_DIM], (1, 2, 0)) * scale_key
    key_cols = jnp.transpose(shaped[:, :, KEY_DIM : 2 * KEY_DIM], (1, 2, 0)) * scale_key
    values = shaped[:, :, 2 * KEY_DIM :]
    upstream = out_flat.reshape(length, local_heads, HEAD_DIM)
    query_feat, query_parts = feature_map(query_cols)
    key_feat, key_parts = feature_map(key_cols)
    feat_count = query_feat.shape[1]
    last_begin = begins[length - 1]
    has_start = (last_begin >= stretch_start).astype(jnp.float32).reshape(1)
    tail_mask = (begins == last_begin).astype(jnp.float32)
    tail_feat = key_feat * tail_mask[None, None, :]
    tail_state = jnp.einsum("hfl,lhe->hfe", tail_feat, values, precision=FAST)
    tail_norm = jnp.sum(tail_feat, axis=2)
    prefix = carried_in(tail_state, tail_norm, has_start, None, "seq", False)
    flags = prefix[2]
    causal = jnp.arange(block_len)[:, None] >= jnp.arange(block_len)[None, :]
    query_blk = jnp.transpose(query_feat.reshape(local_heads, feat_count, blocks, block_len), (2, 0, 1, 3))
    key_blk = jnp.transpose(key_feat.reshape(local_heads, feat_count, blocks, block_len), (2, 0, 1, 3))
    value_blk = values.reshape(blocks, block_len, local_heads, HEAD_DIM)
    doc_blk = begins.reshape(blocks, block_len)
    block_start = stretch_start + jnp.arange(blocks, dtype=jnp.int32) * block_len
    allowed = causal[None] & (doc_blk[:, :, None] == doc_blk[:, None, :])
    from_carry = (doc_blk < block_start[:, None]).astype(jnp.float32)
    block_tail = (doc_blk == doc_blk[:, block_len - 1 :]).astype(jnp.float32)
    breaks = (doc_blk[:, block_len - 1] >= block_start).astype(jnp.int32)
    upto = jnp.cumsum(breaks)
    before = upto - breaks
    order = jnp.arange(blocks)
    ahead_w = ((order[None, :] < order[:, None]) & (before[:, None] == upto[None, :])).astype(jnp.float32)
    ahead_p = (before == 0).astype(jnp.float32)
    behind_w = ((order[None, :] > order[:, None]) & (before[None, :] == upto[:, None])).astype(jnp.float32)
    behind_p = (upto[blocks - 1] == upto).astype(jnp.float32)
    scores = jnp.where(
        allowed[:, None], jnp.einsum("bhft,bhfs->bhts", query_blk, key_blk, precision=FAST), 0.0
    )
    tail_keys = key_blk * block_tail[:, None, None, :]
    tail_states = jnp.einsum("bhfs,bshe->bhfe", tail_keys, value_blk, precision=FAST)
    tail_norms = jnp.sum(tail_keys, axis=3)
    carry_state = jnp.einsum("bc,chfe->bhfe", ahead_w, tail_states, precision=HIGHEST) + ahead_p[
        :, None, None, None
    ] * prefix[0][None]
    carry_norm = jnp.einsum("bc,chf->bhf", ahead_w, tail_norms, precision=HIGHEST) + ahead_p[
        :, None, None
    ] * prefix[1][None]
    numerators = jnp.einsum("bhts,bshe->bthe", scores, value_blk, precision=FAST) + from_carry[
        :, :, None, None
    ] * jnp.einsum("bhft,bhfe->bthe", query_blk, carry_state, precision=FAST)
    denominators = jnp.sum(scores, axis=3) + from_carry[:, None, :] * jnp.einsum(
        "bhft,bhf->bht", query_blk, carry_norm, precision=FAST
    )
    denom_rows = jnp.transpose(denominators, (0, 2, 1)).reshape(length, local_heads)
    attended = numerators.reshape(length, local_heads, HEAD_DIM) / denom_rows[:, :, None]
    grad_num = upstream / denom_rows[:, :, None]
    scalar_grad = -jnp.sum(upstream * attended, axis=2) / denom_rows
    lead_mask = (begins < stretch_start).astype(jnp.float32)
    lead_feat = query_feat * lead_mask[None, None, :]
    lead_state = jnp.einsum("hfl,lhe->hfe", lead_feat, grad_num, precision=FAST)
    lead_norm = jnp.einsum("hfl,lh->hf", lead_feat, scalar_grad, precision=FAST)
    suffix = carried_in(lead_state, lead_norm, jnp.zeros((0,), jnp.float32), flags, "seq", True)
    grad_blk = grad_num.reshape(blocks, block_len, local_heads, HEAD_DIM)
    scalar_cols = jnp.transpose(scalar_grad.reshape(blocks, block_len, local_heads), (0, 2, 1))
    dscores = jnp.where(
        allowed[:, None],
        jnp.einsum("bthe,bshe->bhts", grad_blk, value_blk, precision=FAST)
        + scalar_cols[:, :, :, None],
        0.0,
    )
    lead_blk = query_blk * from_carry[:, None, None, :]
    lead_states = jnp.einsum("bhft,bthe->bhfe", lead_blk, grad_blk, precision=FAST)
    lead_norms = jnp.einsum("bhft,bht->bhf", lead_blk, scalar_cols, precision=FAST)
    back_state = jnp.einsum("bc,chfe->bhfe", behind_w, lead_states, precision=HIGHEST) + behind_p[
        :, None, None, None
    ] * suffix[0][None]
    back_norm = jnp.einsum("bc,chf->bhf", behind_w, lead_norms, precision=HIGHEST) + behind_p[
        :, None, None
    ] * suffix[1][None]
    grad_qblocks = jnp.einsum("bhts,bhfs->bhft", dscores, key_blk, precision=FAST) + from_carry[
        :, None, None, :
    ] * (
        jnp.einsum("bhfe,bthe->bhft", carry_state, grad_blk, precision=FAST)
        + carry_norm[:, :, :, None] * scalar_cols[:, :, None, :]
    )
    grad_kblocks = jnp.einsum("bhts,bhft->bhfs", dscores, query_blk, precision=FAST) + block_tail[
        :, None, None, :
    ] * (
        jnp.einsum("bhfe,bshe->bhfs", back_state, value_blk, precision=FAST)
        + back_norm[:, :, :, None]
    )
    grad_vblocks = jnp.einsum("bhts,bthe->bshe", scores, grad_blk, precision=FAST) + block_tail[
        :, :, None, None
    ] * jnp.einsum("bhfs,bhfe->bshe", key_blk, back_state, precision=FAST)
    query_grad = jnp.transpose(grad_qblocks, (1, 2, 0, 3)).reshape(local_heads, feat_count, length)
    key_grad = jnp.transpose(grad_kblocks, (1, 2, 0, 3)).reshape(local_heads, feat_count, length)
    value_grad = grad_vblocks.reshape(length, local_heads, HEAD_DIM)
    query_in = jnp.transpose(feature_pull(query_parts, query_grad) * scale_key, (2, 0, 1))
    key_in = jnp.transpose(feature_pull(key_parts, key_grad) * scale_key, (2, 0, 1))
    return jnp.concatenate([query_in, key_in, value_grad], axis=2).reshape(
        length, local_heads * head_width
    )


def on_device(projected, out_grads, conv_weight, doc_lengths):
    row_count = projected.shape[0]
    head_count = lax.axis_size("head")
    seq_index = lax.axis_index("seq")
    head_index = lax.axis_index("head")
    group_len = row_count * head_count
    token_base = (seq_index * head_count + head_index) * row_count
    stretch_start = seq_index * group_len
    token_begins, token_offsets = doc_place(doc_lengths, token_base, row_count + 2)
    leading = passed_along(projected[row_count - 2 :], ("seq", "head"), 1)
    outgoing = conv_forward(projected, leading, conv_weight, token_offsets)
    mixed_width = outgoing.shape[1] // head_count
    both = jnp.concatenate(
        [outgoing.reshape(row_count, head_count, -1), out_grads.reshape(row_count, head_count, -1)],
        axis=2,
    ).reshape(row_count, -1)
    landed = lax.all_to_all(both, "head", split_axis=1, concat_axis=0, tiled=True)
    arrived, upstream = (landed[:, :mixed_width], landed[:, mixed_width:])
    group_begins, group_offsets = doc_place(doc_lengths, stretch_start, group_len + 2)
    grad_mixed = attention_grads(arrived, upstream, group_begins[:group_len], stretch_start)
    returned = lax.all_to_all(grad_mixed, "head", split_axis=0, concat_axis=1, tiled=True)
    trailing = passed_along(returned[:2], ("seq", "head"), -1)
    grad_projected, weight_part = conv_backward(
        returned, trailing, projected, leading, conv_weight, token_offsets
    )
    grad_conv = lax.psum(weight_part, ("seq", "head"))
    return (grad_projected, grad_conv)


def solution(mesh):
    return jax.shard_map(
        on_device,
        mesh=mesh,
        in_specs=(P(("seq", "head"), None), P(("seq", "head"), None), P(), P()),
        out_specs=(P(("seq", "head"), None), P()),
        check_vma=False,
    )
```

```python
import math

import jax
import jax.numpy as jnp
import numpy as np
from jax import lax
from jax.sharding import PartitionSpec as P

KEY_DIM = 16
HEAD_DIM = 128


HIGHEST = lax.Precision.HIGHEST


def carried_in(state, norm, flag, axis, reverse):
    count = lax.axis_size(axis)
    step = -1 if reverse else 1
    size = state.size
    packed = jnp.concatenate([state.reshape(-1), norm.reshape(-1), flag])
    width = 128
    padded = jnp.pad(packed, (0, -packed.shape[0] % width)).reshape(-1, width)
    at_flag = divmod(packed.shape[0] - 1, width)

    def shifted(rows, distance):
        pairs = [(s, s + distance * step) for s in range(count) if 0 <= s + distance * step < count]
        return lax.ppermute(rows, axis, pairs)

    acc = shifted(padded, 1)
    distance = 1
    while distance < count:
        earlier = shifted(acc, distance)
        acc = acc + (1.0 - acc[at_flag]) * earlier
        distance *= 2
    total = acc.reshape(-1)
    return (total[:size].reshape(state.shape), total[size : size + norm.size].reshape(norm.shape))


def passed_along(value, axis, steps):
    count = lax.axis_size(axis)
    initial, last = (max(0, -steps), min(count, count - steps))
    return lax.ppermute(value, axis, [(source, source + steps) for source in range(initial, last)])


def pair_pickers(key_size):
    upper_i, upper_j = np.triu_indices(key_size)
    factors = np.where(upper_i == upper_j, 1.0 / math.sqrt(2.0), 1.0).astype(np.float32)
    eye = np.eye(key_size, dtype=np.float32)
    return (jnp.asarray(eye[upper_i]), jnp.asarray(eye[upper_j]), jnp.asarray(factors))


def feature_map(columns):
    pick_i, pick_j, factors = pair_pickers(columns.shape[1])
    first = jnp.einsum("pk,hkl->hpl", pick_i, columns, precision=HIGHEST)
    second = jnp.einsum("pk,hkl->hpl", pick_j, columns, precision=HIGHEST)
    products = first * second * factors[None, :, None]
    constant = jnp.ones((columns.shape[0], 1, columns.shape[2]), jnp.float32)
    return (jnp.concatenate([constant, columns, products], axis=1), (first, second))


def feature_pull(parts, grad):
    first, second = parts
    key_size = KEY_DIM
    pick_i, pick_j, factors = pair_pickers(key_size)
    pair_grad = grad[:, 1 + key_size :] * factors[None, :, None]
    return (
        grad[:, 1 : 1 + key_size]
        + jnp.einsum("pk,hpl->hkl", pick_i, pair_grad * second, precision=HIGHEST)
        + jnp.einsum("pk,hpl->hkl", pick_j, pair_grad * first, precision=HIGHEST)
    )


def doc_place(doc_lengths, anchor, amount):
    positions = anchor + jnp.arange(amount, dtype=jnp.int32)
    starts = jnp.cumsum(doc_lengths) - doc_lengths
    begins = jnp.max(jnp.where(starts[None, :] <= positions[:, None], starts[None, :], 0), axis=1)
    return (begins, positions - begins)


def conv_forward(signal, leading, weights, offsets):
    row_count = signal.shape[0]
    behind = jnp.concatenate([leading, signal], axis=0)
    back_one = behind[1 : row_count + 1] * (offsets[0:row_count] >= 1).astype(jnp.float32)[:, None]
    back_two = behind[0:row_count] * (offsets[0:row_count] >= 2).astype(jnp.float32)[:, None]
    return weights[0] * signal + weights[1] * back_one + weights[2] * back_two


def conv_backward(grad_rows, trailing, signal, leading, weights, offsets):
    row_count = grad_rows.shape[0]
    ahead_rows = jnp.concatenate([grad_rows, trailing], axis=0)
    ahead_one = (
        ahead_rows[1 : row_count + 1]
        * (offsets[1 : row_count + 1] >= 1).astype(jnp.float32)[:, None]
    )
    ahead_two = (
        ahead_rows[2 : row_count + 2]
        * (offsets[2 : row_count + 2] >= 2).astype(jnp.float32)[:, None]
    )
    grad_signal = weights[0] * grad_rows + weights[1] * ahead_one + weights[2] * ahead_two
    behind = jnp.concatenate([leading, signal], axis=0)
    own_one = (offsets[0:row_count] >= 1).astype(jnp.float32)[:, None]
    own_two = (offsets[0:row_count] >= 2).astype(jnp.float32)[:, None]
    grad_weights = jnp.stack(
        [
            jnp.sum(grad_rows * signal, axis=0),
            jnp.sum(grad_rows * behind[1 : row_count + 1] * own_one, axis=0),
            jnp.sum(grad_rows * behind[0:row_count] * own_two, axis=0),
        ],
        axis=0,
    )
    return (grad_signal, grad_weights)


def attention_grads(mixed_rows, out_flat, begins, stretch_start):
    length = mixed_rows.shape[0]
    head_width = 2 * KEY_DIM + HEAD_DIM
    local_heads = mixed_rows.shape[1] // head_width
    block_len = min(128, length)
    blocks = length // block_len
    scale_key = KEY_DIM ** (-0.25)
    shaped = mixed_rows.reshape(length, local_heads, head_width)
    query_cols = jnp.transpose(shaped[:, :, :KEY_DIM], (1, 2, 0)) * scale_key
    key_cols = jnp.transpose(shaped[:, :, KEY_DIM : 2 * KEY_DIM], (1, 2, 0)) * scale_key
    values = shaped[:, :, 2 * KEY_DIM :]
    upstream = out_flat.reshape(length, local_heads, HEAD_DIM)
    query_feat, query_parts = feature_map(query_cols)
    key_feat, key_parts = feature_map(key_cols)
    feat_count = query_feat.shape[1]
    last_begin = begins[length - 1]
    has_start = (last_begin >= stretch_start).astype(jnp.float32).reshape(1)
    tail_mask = (begins == last_begin).astype(jnp.float32)
    tail_feat = key_feat * tail_mask[None, None, :]
    tail_state = jnp.einsum("hfl,lhe->hfe", tail_feat, values, precision=HIGHEST)
    tail_norm = jnp.sum(tail_feat, axis=2)
    prefix = carried_in(tail_state, tail_norm, has_start, "seq", False)
    causal = jnp.arange(block_len)[:, None] >= jnp.arange(block_len)[None, :]
    query_blk = jnp.transpose(query_feat.reshape(local_heads, feat_count, blocks, block_len), (2, 0, 1, 3))
    key_blk = jnp.transpose(key_feat.reshape(local_heads, feat_count, blocks, block_len), (2, 0, 1, 3))
    value_blk = values.reshape(blocks, block_len, local_heads, HEAD_DIM)
    doc_blk = begins.reshape(blocks, block_len)
    block_start = stretch_start + jnp.arange(blocks, dtype=jnp.int32) * block_len
    allowed = causal[None] & (doc_blk[:, :, None] == doc_blk[:, None, :])
    from_carry = (doc_blk < block_start[:, None]).astype(jnp.float32)
    block_tail = (doc_blk == doc_blk[:, block_len - 1 :]).astype(jnp.float32)
    breaks = (doc_blk[:, block_len - 1] >= block_start).astype(jnp.int32)
    upto = jnp.cumsum(breaks)
    before = upto - breaks
    order = jnp.arange(blocks)
    ahead_w = ((order[None, :] < order[:, None]) & (before[:, None] == upto[None, :])).astype(jnp.float32)
    ahead_p = (before == 0).astype(jnp.float32)
    behind_w = ((order[None, :] > order[:, None]) & (before[None, :] == upto[:, None])).astype(jnp.float32)
    behind_p = (upto[blocks - 1] == upto).astype(jnp.float32)
    scores = jnp.where(
        allowed[:, None], jnp.einsum("bhft,bhfs->bhts", query_blk, key_blk, precision=HIGHEST), 0.0
    )
    tail_keys = key_blk * block_tail[:, None, None, :]
    tail_states = jnp.einsum("bhfs,bshe->bhfe", tail_keys, value_blk, precision=HIGHEST)
    tail_norms = jnp.sum(tail_keys, axis=3)
    carry_state = jnp.einsum("bc,chfe->bhfe", ahead_w, tail_states, precision=HIGHEST) + ahead_p[
        :, None, None, None
    ] * prefix[0][None]
    carry_norm = jnp.einsum("bc,chf->bhf", ahead_w, tail_norms, precision=HIGHEST) + ahead_p[
        :, None, None
    ] * prefix[1][None]
    numerators = jnp.einsum("bhts,bshe->bthe", scores, value_blk, precision=HIGHEST) + from_carry[
        :, :, None, None
    ] * jnp.einsum("bhft,bhfe->bthe", query_blk, carry_state, precision=HIGHEST)
    denominators = jnp.sum(scores, axis=3) + from_carry[:, None, :] * jnp.einsum(
        "bhft,bhf->bht", query_blk, carry_norm, precision=HIGHEST
    )
    denom_rows = jnp.transpose(denominators, (0, 2, 1)).reshape(length, local_heads)
    attended = numerators.reshape(length, local_heads, HEAD_DIM) / denom_rows[:, :, None]
    grad_num = upstream / denom_rows[:, :, None]
    scalar_grad = -jnp.sum(upstream * attended, axis=2) / denom_rows
    lead_mask = (begins < stretch_start).astype(jnp.float32)
    lead_feat = query_feat * lead_mask[None, None, :]
    lead_state = jnp.einsum("hfl,lhe->hfe", lead_feat, grad_num, precision=HIGHEST)
    lead_norm = jnp.einsum("hfl,lh->hf", lead_feat, scalar_grad, precision=HIGHEST)
    suffix = carried_in(lead_state, lead_norm, has_start, "seq", True)
    grad_blk = grad_num.reshape(blocks, block_len, local_heads, HEAD_DIM)
    scalar_cols = jnp.transpose(scalar_grad.reshape(blocks, block_len, local_heads), (0, 2, 1))
    dscores = jnp.where(
        allowed[:, None],
        jnp.einsum("bthe,bshe->bhts", grad_blk, value_blk, precision=HIGHEST)
        + scalar_cols[:, :, :, None],
        0.0,
    )
    lead_blk = query_blk * from_carry[:, None, None, :]
    lead_states = jnp.einsum("bhft,bthe->bhfe", lead_blk, grad_blk, precision=HIGHEST)
    lead_norms = jnp.einsum("bhft,bht->bhf", lead_blk, scalar_cols, precision=HIGHEST)
    back_state = jnp.einsum("bc,chfe->bhfe", behind_w, lead_states, precision=HIGHEST) + behind_p[
        :, None, None, None
    ] * suffix[0][None]
    back_norm = jnp.einsum("bc,chf->bhf", behind_w, lead_norms, precision=HIGHEST) + behind_p[
        :, None, None
    ] * suffix[1][None]
    grad_qblocks = jnp.einsum("bhts,bhfs->bhft", dscores, key_blk, precision=HIGHEST) + from_carry[
        :, None, None, :
    ] * (
        jnp.einsum("bhfe,bthe->bhft", carry_state, grad_blk, precision=HIGHEST)
        + carry_norm[:, :, :, None] * scalar_cols[:, :, None, :]
    )
    grad_kblocks = jnp.einsum("bhts,bhft->bhfs", dscores, query_blk, precision=HIGHEST) + block_tail[
        :, None, None, :
    ] * (
        jnp.einsum("bhfe,bshe->bhfs", back_state, value_blk, precision=HIGHEST)
        + back_norm[:, :, :, None]
    )
    grad_vblocks = jnp.einsum("bhts,bthe->bshe", scores, grad_blk, precision=HIGHEST) + block_tail[
        :, :, None, None
    ] * jnp.einsum("bhfs,bhfe->bshe", key_blk, back_state, precision=HIGHEST)
    query_grad = jnp.transpose(grad_qblocks, (1, 2, 0, 3)).reshape(local_heads, feat_count, length)
    key_grad = jnp.transpose(grad_kblocks, (1, 2, 0, 3)).reshape(local_heads, feat_count, length)
    value_grad = grad_vblocks.reshape(length, local_heads, HEAD_DIM)
    query_in = jnp.transpose(feature_pull(query_parts, query_grad) * scale_key, (2, 0, 1))
    key_in = jnp.transpose(feature_pull(key_parts, key_grad) * scale_key, (2, 0, 1))
    return jnp.concatenate([query_in, key_in, value_grad], axis=2).reshape(
        length, local_heads * head_width
    )


def on_device(projected, out_grads, conv_weight, doc_lengths):
    row_count = projected.shape[0]
    head_count = lax.axis_size("head")
    seq_index = lax.axis_index("seq")
    head_index = lax.axis_index("head")
    group_len = row_count * head_count
    token_base = (seq_index * head_count + head_index) * row_count
    stretch_start = seq_index * group_len
    token_begins, token_offsets = doc_place(doc_lengths, token_base, row_count + 2)
    leading = passed_along(projected[row_count - 2 :], ("seq", "head"), 1)
    outgoing = conv_forward(projected, leading, conv_weight, token_offsets)
    arrived, upstream = (
        lax.all_to_all(outgoing, "head", split_axis=1, concat_axis=0, tiled=True),
        lax.all_to_all(out_grads, "head", split_axis=1, concat_axis=0, tiled=True),
    )
    group_begins, group_offsets = doc_place(doc_lengths, stretch_start, group_len + 2)
    grad_mixed = attention_grads(arrived, upstream, group_begins[:group_len], stretch_start)
    returned = lax.all_to_all(grad_mixed, "head", split_axis=0, concat_axis=1, tiled=True)
    trailing = passed_along(returned[:2], ("seq", "head"), -1)
    grad_projected, weight_part = conv_backward(
        returned, trailing, projected, leading, conv_weight, token_offsets
    )
    grad_conv = lax.psum(weight_part, ("seq", "head"))
    return (grad_projected, grad_conv)


def solution(mesh):
    return jax.shard_map(
        on_device,
        mesh=mesh,
        in_specs=(P(("seq", "head"), None), P(("seq", "head"), None), P(), P()),
        out_specs=(P(("seq", "head"), None), P()),
        check_vma=False,
    )
```

```python
import math

import jax
import jax.numpy as jnp
import numpy as np
from jax import lax
from jax.sharding import PartitionSpec as P

KEY_DIM = 16
HEAD_DIM = 128


HIGHEST = lax.Precision.HIGHEST


def carried_in(state, norm, flag, axis, reverse):
    count = lax.axis_size(axis)
    step = -1 if reverse else 1
    size = state.size
    packed = jnp.concatenate([state.reshape(-1), norm.reshape(-1), flag])
    width = 128
    padded = jnp.pad(packed, (0, -packed.shape[0] % width)).reshape(-1, width)
    at_flag = divmod(packed.shape[0] - 1, width)

    def shifted(rows, distance):
        pairs = [(s, s + distance * step) for s in range(count) if 0 <= s + distance * step < count]
        return lax.ppermute(rows, axis, pairs)

    acc = shifted(padded, 1)
    distance = 1
    while distance < count:
        earlier = shifted(acc, distance)
        acc = acc + (1.0 - acc[at_flag]) * earlier
        distance *= 2
    total = acc.reshape(-1)
    return (total[:size].reshape(state.shape), total[size : size + norm.size].reshape(norm.shape))


def passed_along(value, axis, steps):
    count = lax.axis_size(axis)
    initial, last = (max(0, -steps), min(count, count - steps))
    return lax.ppermute(value, axis, [(source, source + steps) for source in range(initial, last)])


def pair_pickers(key_size):
    upper_i, upper_j = np.triu_indices(key_size)
    factors = np.where(upper_i == upper_j, 1.0 / math.sqrt(2.0), 1.0).astype(np.float32)
    eye = np.eye(key_size, dtype=np.float32)
    return (jnp.asarray(eye[upper_i]), jnp.asarray(eye[upper_j]), jnp.asarray(factors))


def feature_map(columns):
    pick_i, pick_j, factors = pair_pickers(columns.shape[1])
    first = jnp.einsum("pk,hkl->hpl", pick_i, columns, precision=HIGHEST)
    second = jnp.einsum("pk,hkl->hpl", pick_j, columns, precision=HIGHEST)
    products = first * second * factors[None, :, None]
    constant = jnp.ones((columns.shape[0], 1, columns.shape[2]), jnp.float32)
    return (jnp.concatenate([constant, columns, products], axis=1), (first, second))


def feature_pull(parts, grad):
    first, second = parts
    key_size = KEY_DIM
    pick_i, pick_j, factors = pair_pickers(key_size)
    pair_grad = grad[:, 1 + key_size :] * factors[None, :, None]
    return (
        grad[:, 1 : 1 + key_size]
        + jnp.einsum("pk,hpl->hkl", pick_i, pair_grad * second, precision=HIGHEST)
        + jnp.einsum("pk,hpl->hkl", pick_j, pair_grad * first, precision=HIGHEST)
    )


def doc_place(doc_lengths, anchor, amount):
    positions = anchor + jnp.arange(amount, dtype=jnp.int32)
    starts = jnp.cumsum(doc_lengths) - doc_lengths
    begins = jnp.max(jnp.where(starts[None, :] <= positions[:, None], starts[None, :], 0), axis=1)
    return (begins, positions - begins)


def conv_forward(signal, leading, weights, offsets):
    row_count = signal.shape[0]
    behind = jnp.concatenate([leading, signal], axis=0)
    back_one = behind[1 : row_count + 1] * (offsets[0:row_count] >= 1).astype(jnp.float32)[:, None]
    back_two = behind[0:row_count] * (offsets[0:row_count] >= 2).astype(jnp.float32)[:, None]
    return weights[0] * signal + weights[1] * back_one + weights[2] * back_two


def conv_backward(grad_rows, trailing, signal, leading, weights, offsets):
    row_count = grad_rows.shape[0]
    ahead_rows = jnp.concatenate([grad_rows, trailing], axis=0)
    ahead_one = (
        ahead_rows[1 : row_count + 1]
        * (offsets[1 : row_count + 1] >= 1).astype(jnp.float32)[:, None]
    )
    ahead_two = (
        ahead_rows[2 : row_count + 2]
        * (offsets[2 : row_count + 2] >= 2).astype(jnp.float32)[:, None]
    )
    grad_signal = weights[0] * grad_rows + weights[1] * ahead_one + weights[2] * ahead_two
    behind = jnp.concatenate([leading, signal], axis=0)
    own_one = (offsets[0:row_count] >= 1).astype(jnp.float32)[:, None]
    own_two = (offsets[0:row_count] >= 2).astype(jnp.float32)[:, None]
    grad_weights = jnp.stack(
        [
            jnp.sum(grad_rows * signal, axis=0),
            jnp.sum(grad_rows * behind[1 : row_count + 1] * own_one, axis=0),
            jnp.sum(grad_rows * behind[0:row_count] * own_two, axis=0),
        ],
        axis=0,
    )
    return (grad_signal, grad_weights)


def attention_grads(mixed_rows, out_flat, begins, stretch_start):
    length = mixed_rows.shape[0]
    head_width = 2 * KEY_DIM + HEAD_DIM
    local_heads = mixed_rows.shape[1] // head_width
    block_len = min(128, length)
    blocks = length // block_len
    scale_key = KEY_DIM ** (-0.25)
    shaped = mixed_rows.reshape(length, local_heads, head_width)
    query_cols = jnp.transpose(shaped[:, :, :KEY_DIM], (1, 2, 0)) * scale_key
    key_cols = jnp.transpose(shaped[:, :, KEY_DIM : 2 * KEY_DIM], (1, 2, 0)) * scale_key
    values = shaped[:, :, 2 * KEY_DIM :]
    upstream = out_flat.reshape(length, local_heads, HEAD_DIM)
    query_feat, query_parts = feature_map(query_cols)
    key_feat, key_parts = feature_map(key_cols)
    feat_count = query_feat.shape[1]
    last_begin = begins[length - 1]
    has_start = (last_begin >= stretch_start).astype(jnp.float32).reshape(1)
    tail_mask = (begins == last_begin).astype(jnp.float32)
    tail_feat = key_feat * tail_mask[None, None, :]
    tail_state = jnp.einsum("hfl,lhe->hfe", tail_feat, values, precision=HIGHEST)
    tail_norm = jnp.sum(tail_feat, axis=2)
    prefix = carried_in(tail_state, tail_norm, has_start, "seq", False)
    causal = jnp.arange(block_len)[:, None] >= jnp.arange(block_len)[None, :]
    query_blk = jnp.transpose(query_feat.reshape(local_heads, feat_count, blocks, block_len), (2, 0, 1, 3))
    key_blk = jnp.transpose(key_feat.reshape(local_heads, feat_count, blocks, block_len), (2, 0, 1, 3))
    value_blk = values.reshape(blocks, block_len, local_heads, HEAD_DIM)
    doc_blk = begins.reshape(blocks, block_len)
    block_start = stretch_start + jnp.arange(blocks, dtype=jnp.int32) * block_len
    allowed = causal[None] & (doc_blk[:, :, None] == doc_blk[:, None, :])
    from_carry = (doc_blk < block_start[:, None]).astype(jnp.float32)
    block_tail = (doc_blk == doc_blk[:, block_len - 1 :]).astype(jnp.float32)
    breaks = (doc_blk[:, block_len - 1] >= block_start).astype(jnp.int32)
    upto = jnp.cumsum(breaks)
    before = upto - breaks
    order = jnp.arange(blocks)
    ahead_w = ((order[None, :] < order[:, None]) & (before[:, None] == upto[None, :])).astype(jnp.float32)
    ahead_p = (before == 0).astype(jnp.float32)
    behind_w = ((order[None, :] > order[:, None]) & (before[None, :] == upto[:, None])).astype(jnp.float32)
    behind_p = (upto[blocks - 1] == upto).astype(jnp.float32)
    scores = jnp.where(
        allowed[:, None], jnp.einsum("bhft,bhfs->bhts", query_blk, key_blk, precision=HIGHEST), 0.0
    )
    tail_keys = key_blk * block_tail[:, None, None, :]
    tail_states = jnp.einsum("bhfs,bshe->bhfe", tail_keys, value_blk, precision=HIGHEST)
    tail_norms = jnp.sum(tail_keys, axis=3)
    carry_state = jnp.einsum("bc,chfe->bhfe", ahead_w, tail_states, precision=HIGHEST) + ahead_p[
        :, None, None, None
    ] * prefix[0][None]
    carry_norm = jnp.einsum("bc,chf->bhf", ahead_w, tail_norms, precision=HIGHEST) + ahead_p[
        :, None, None
    ] * prefix[1][None]
    numerators = jnp.einsum("bhts,bshe->bthe", scores, value_blk, precision=HIGHEST) + from_carry[
        :, :, None, None
    ] * jnp.einsum("bhft,bhfe->bthe", query_blk, carry_state, precision=HIGHEST)
    denominators = jnp.sum(scores, axis=3) + from_carry[:, None, :] * jnp.einsum(
        "bhft,bhf->bht", query_blk, carry_norm, precision=HIGHEST
    )
    denom_rows = jnp.transpose(denominators, (0, 2, 1)).reshape(length, local_heads)
    attended = numerators.reshape(length, local_heads, HEAD_DIM) / denom_rows[:, :, None]
    grad_num = upstream / denom_rows[:, :, None]
    scalar_grad = -jnp.sum(upstream * attended, axis=2) / denom_rows
    lead_mask = (begins < stretch_start).astype(jnp.float32)
    lead_feat = query_feat * lead_mask[None, None, :]
    lead_state = jnp.einsum("hfl,lhe->hfe", lead_feat, grad_num, precision=HIGHEST)
    lead_norm = jnp.einsum("hfl,lh->hf", lead_feat, scalar_grad, precision=HIGHEST)
    suffix = carried_in(lead_state, lead_norm, has_start, "seq", True)
    grad_blk = grad_num.reshape(blocks, block_len, local_heads, HEAD_DIM)
    scalar_cols = jnp.transpose(scalar_grad.reshape(blocks, block_len, local_heads), (0, 2, 1))
    dscores = jnp.where(
        allowed[:, None],
        jnp.einsum("bthe,bshe->bhts", grad_blk, value_blk, precision=HIGHEST)
        + scalar_cols[:, :, :, None],
        0.0,
    )
    lead_blk = query_blk * from_carry[:, None, None, :]
    lead_states = jnp.einsum("bhft,bthe->bhfe", lead_blk, grad_blk, precision=HIGHEST)
    lead_norms = jnp.einsum("bhft,bht->bhf", lead_blk, scalar_cols, precision=HIGHEST)
    back_state = jnp.einsum("bc,chfe->bhfe", behind_w, lead_states, precision=HIGHEST) + behind_p[
        :, None, None, None
    ] * suffix[0][None]
    back_norm = jnp.einsum("bc,chf->bhf", behind_w, lead_norms, precision=HIGHEST) + behind_p[
        :, None, None
    ] * suffix[1][None]
    grad_qblocks = jnp.einsum("bhts,bhfs->bhft", dscores, key_blk, precision=HIGHEST) + from_carry[
        :, None, None, :
    ] * (
        jnp.einsum("bhfe,bthe->bhft", carry_state, grad_blk, precision=HIGHEST)
        + carry_norm[:, :, :, None] * scalar_cols[:, :, None, :]
    )
    grad_kblocks = jnp.einsum("bhts,bhft->bhfs", dscores, query_blk, precision=HIGHEST) + block_tail[
        :, None, None, :
    ] * (
        jnp.einsum("bhfe,bshe->bhfs", back_state, value_blk, precision=HIGHEST)
        + back_norm[:, :, :, None]
    )
    grad_vblocks = jnp.einsum("bhts,bthe->bshe", scores, grad_blk, precision=HIGHEST) + block_tail[
        :, :, None, None
    ] * jnp.einsum("bhfs,bhfe->bshe", key_blk, back_state, precision=HIGHEST)
    query_grad = jnp.transpose(grad_qblocks, (1, 2, 0, 3)).reshape(local_heads, feat_count, length)
    key_grad = jnp.transpose(grad_kblocks, (1, 2, 0, 3)).reshape(local_heads, feat_count, length)
    value_grad = grad_vblocks.reshape(length, local_heads, HEAD_DIM)
    query_in = jnp.transpose(feature_pull(query_parts, query_grad) * scale_key, (2, 0, 1))
    key_in = jnp.transpose(feature_pull(key_parts, key_grad) * scale_key, (2, 0, 1))
    return jnp.concatenate([query_in, key_in, value_grad], axis=2).reshape(
        length, local_heads * head_width
    )


def summed_everywhere(part, axes):
    count = math.prod(lax.axis_size(axis) for axis in axes)
    distance = 1
    while distance < count:
        part = part + lax.ppermute(part, axes, [(s, s ^ distance) for s in range(count)])
        distance *= 2
    return part


def on_device(projected, out_grads, conv_weight, doc_lengths):
    row_count = projected.shape[0]
    head_count = lax.axis_size("head")
    seq_index = lax.axis_index("seq")
    head_index = lax.axis_index("head")
    group_len = row_count * head_count
    token_base = (seq_index * head_count + head_index) * row_count
    stretch_start = seq_index * group_len
    token_begins, token_offsets = doc_place(doc_lengths, token_base, row_count + 2)
    leading = passed_along(projected[row_count - 2 :], ("seq", "head"), 1)
    outgoing = conv_forward(projected, leading, conv_weight, token_offsets)
    arrived, upstream = (
        lax.all_to_all(outgoing, "head", split_axis=1, concat_axis=0, tiled=True),
        lax.all_to_all(out_grads, "head", split_axis=1, concat_axis=0, tiled=True),
    )
    group_begins, group_offsets = doc_place(doc_lengths, stretch_start, group_len + 2)
    grad_mixed = attention_grads(arrived, upstream, group_begins[:group_len], stretch_start)
    returned = lax.all_to_all(grad_mixed, "head", split_axis=0, concat_axis=1, tiled=True)
    trailing = passed_along(returned[:2], ("seq", "head"), -1)
    grad_projected, weight_part = conv_backward(
        returned, trailing, projected, leading, conv_weight, token_offsets
    )
    grad_conv = summed_everywhere(weight_part, ("seq", "head"))
    return (grad_projected, grad_conv)


def solution(mesh):
    return jax.shard_map(
        on_device,
        mesh=mesh,
        in_specs=(P(("seq", "head"), None), P(("seq", "head"), None), P(), P()),
        out_specs=(P(("seq", "head"), None), P()),
        check_vma=False,
    )
```

```python
import math

import jax
import jax.numpy as jnp
import numpy as np
from jax import lax
from jax.sharding import PartitionSpec as P

KEY_DIM = 16
HEAD_DIM = 128


HIGHEST = lax.Precision.HIGHEST


def carried_in(state, norm, flag, axis, reverse):
    count = lax.axis_size(axis)
    step = -1 if reverse else 1
    size = state.size
    packed = jnp.concatenate([state.reshape(-1), norm.reshape(-1), flag])
    width = 128
    padded = jnp.pad(packed, (0, -packed.shape[0] % width)).reshape(-1, width)
    at_flag = divmod(packed.shape[0] - 1, width)

    def shifted(rows, distance):
        pairs = [(s, s + distance * step) for s in range(count) if 0 <= s + distance * step < count]
        return lax.ppermute(rows, axis, pairs)

    acc = shifted(padded, 1)
    distance = 1
    if count > 2:
        second = shifted(padded, 2)
        acc = acc + (1.0 - acc[at_flag]) * second
        distance = 2
    while distance < count:
        earlier = shifted(acc, distance)
        acc = acc + (1.0 - acc[at_flag]) * earlier
        distance *= 2
    total = acc.reshape(-1)
    return (total[:size].reshape(state.shape), total[size : size + norm.size].reshape(norm.shape))


def passed_along(value, axis, steps):
    count = lax.axis_size(axis)
    initial, last = (max(0, -steps), min(count, count - steps))
    return lax.ppermute(value, axis, [(source, source + steps) for source in range(initial, last)])


def pair_pickers(key_size):
    upper_i, upper_j = np.triu_indices(key_size)
    factors = np.where(upper_i == upper_j, 1.0 / math.sqrt(2.0), 1.0).astype(np.float32)
    eye = np.eye(key_size, dtype=np.float32)
    return (jnp.asarray(eye[upper_i]), jnp.asarray(eye[upper_j]), jnp.asarray(factors))


def feature_map(columns):
    pick_i, pick_j, factors = pair_pickers(columns.shape[1])
    first = jnp.einsum("pk,hkl->hpl", pick_i, columns, precision=HIGHEST)
    second = jnp.einsum("pk,hkl->hpl", pick_j, columns, precision=HIGHEST)
    products = first * second * factors[None, :, None]
    constant = jnp.ones((columns.shape[0], 1, columns.shape[2]), jnp.float32)
    return (jnp.concatenate([constant, columns, products], axis=1), (first, second))


def feature_pull(parts, grad):
    first, second = parts
    key_size = KEY_DIM
    pick_i, pick_j, factors = pair_pickers(key_size)
    pair_grad = grad[:, 1 + key_size :] * factors[None, :, None]
    return (
        grad[:, 1 : 1 + key_size]
        + jnp.einsum("pk,hpl->hkl", pick_i, pair_grad * second, precision=HIGHEST)
        + jnp.einsum("pk,hpl->hkl", pick_j, pair_grad * first, precision=HIGHEST)
    )


def doc_place(doc_lengths, anchor, amount):
    positions = anchor + jnp.arange(amount, dtype=jnp.int32)
    starts = jnp.cumsum(doc_lengths) - doc_lengths
    begins = jnp.max(jnp.where(starts[None, :] <= positions[:, None], starts[None, :], 0), axis=1)
    return (begins, positions - begins)


def conv_forward(signal, leading, weights, offsets):
    row_count = signal.shape[0]
    behind = jnp.concatenate([leading, signal], axis=0)
    back_one = behind[1 : row_count + 1] * (offsets[0:row_count] >= 1).astype(jnp.float32)[:, None]
    back_two = behind[0:row_count] * (offsets[0:row_count] >= 2).astype(jnp.float32)[:, None]
    return weights[0] * signal + weights[1] * back_one + weights[2] * back_two


def conv_backward(grad_rows, trailing, signal, leading, weights, offsets):
    row_count = grad_rows.shape[0]
    ahead_rows = jnp.concatenate([grad_rows, trailing], axis=0)
    ahead_one = (
        ahead_rows[1 : row_count + 1]
        * (offsets[1 : row_count + 1] >= 1).astype(jnp.float32)[:, None]
    )
    ahead_two = (
        ahead_rows[2 : row_count + 2]
        * (offsets[2 : row_count + 2] >= 2).astype(jnp.float32)[:, None]
    )
    grad_signal = weights[0] * grad_rows + weights[1] * ahead_one + weights[2] * ahead_two
    behind = jnp.concatenate([leading, signal], axis=0)
    own_one = (offsets[0:row_count] >= 1).astype(jnp.float32)[:, None]
    own_two = (offsets[0:row_count] >= 2).astype(jnp.float32)[:, None]
    grad_weights = jnp.stack(
        [
            jnp.sum(grad_rows * signal, axis=0),
            jnp.sum(grad_rows * behind[1 : row_count + 1] * own_one, axis=0),
            jnp.sum(grad_rows * behind[0:row_count] * own_two, axis=0),
        ],
        axis=0,
    )
    return (grad_signal, grad_weights)


def attention_grads(mixed_rows, out_flat, begins, stretch_start):
    length = mixed_rows.shape[0]
    head_width = 2 * KEY_DIM + HEAD_DIM
    local_heads = mixed_rows.shape[1] // head_width
    block_len = min(128, length)
    blocks = length // block_len
    scale_key = KEY_DIM ** (-0.25)
    shaped = mixed_rows.reshape(length, local_heads, head_width)
    query_cols = jnp.transpose(shaped[:, :, :KEY_DIM], (1, 2, 0)) * scale_key
    key_cols = jnp.transpose(shaped[:, :, KEY_DIM : 2 * KEY_DIM], (1, 2, 0)) * scale_key
    values = shaped[:, :, 2 * KEY_DIM :]
    upstream = out_flat.reshape(length, local_heads, HEAD_DIM)
    query_feat, query_parts = feature_map(query_cols)
    key_feat, key_parts = feature_map(key_cols)
    feat_count = query_feat.shape[1]
    last_begin = begins[length - 1]
    has_start = (last_begin >= stretch_start).astype(jnp.float32).reshape(1)
    tail_mask = (begins == last_begin).astype(jnp.float32)
    tail_feat = key_feat * tail_mask[None, None, :]
    tail_state = jnp.einsum("hfl,lhe->hfe", tail_feat, values, precision=HIGHEST)
    tail_norm = jnp.sum(tail_feat, axis=2)
    prefix = carried_in(tail_state, tail_norm, has_start, "seq", False)
    causal = jnp.arange(block_len)[:, None] >= jnp.arange(block_len)[None, :]
    query_blk = jnp.transpose(query_feat.reshape(local_heads, feat_count, blocks, block_len), (2, 0, 1, 3))
    key_blk = jnp.transpose(key_feat.reshape(local_heads, feat_count, blocks, block_len), (2, 0, 1, 3))
    value_blk = values.reshape(blocks, block_len, local_heads, HEAD_DIM)
    doc_blk = begins.reshape(blocks, block_len)
    block_start = stretch_start + jnp.arange(blocks, dtype=jnp.int32) * block_len
    allowed = causal[None] & (doc_blk[:, :, None] == doc_blk[:, None, :])
    from_carry = (doc_blk < block_start[:, None]).astype(jnp.float32)
    block_tail = (doc_blk == doc_blk[:, block_len - 1 :]).astype(jnp.float32)
    breaks = (doc_blk[:, block_len - 1] >= block_start).astype(jnp.int32)
    upto = jnp.cumsum(breaks)
    before = upto - breaks
    order = jnp.arange(blocks)
    ahead_w = ((order[None, :] < order[:, None]) & (before[:, None] == upto[None, :])).astype(jnp.float32)
    ahead_p = (before == 0).astype(jnp.float32)
    behind_w = ((order[None, :] > order[:, None]) & (before[None, :] == upto[:, None])).astype(jnp.float32)
    behind_p = (upto[blocks - 1] == upto).astype(jnp.float32)
    scores = jnp.where(
        allowed[:, None], jnp.einsum("bhft,bhfs->bhts", query_blk, key_blk, precision=HIGHEST), 0.0
    )
    tail_keys = key_blk * block_tail[:, None, None, :]
    tail_states = jnp.einsum("bhfs,bshe->bhfe", tail_keys, value_blk, precision=HIGHEST)
    tail_norms = jnp.sum(tail_keys, axis=3)
    carry_state = jnp.einsum("bc,chfe->bhfe", ahead_w, tail_states, precision=HIGHEST) + ahead_p[
        :, None, None, None
    ] * prefix[0][None]
    carry_norm = jnp.einsum("bc,chf->bhf", ahead_w, tail_norms, precision=HIGHEST) + ahead_p[
        :, None, None
    ] * prefix[1][None]
    numerators = jnp.einsum("bhts,bshe->bthe", scores, value_blk, precision=HIGHEST) + from_carry[
        :, :, None, None
    ] * jnp.einsum("bhft,bhfe->bthe", query_blk, carry_state, precision=HIGHEST)
    denominators = jnp.sum(scores, axis=3) + from_carry[:, None, :] * jnp.einsum(
        "bhft,bhf->bht", query_blk, carry_norm, precision=HIGHEST
    )
    denom_rows = jnp.transpose(denominators, (0, 2, 1)).reshape(length, local_heads)
    attended = numerators.reshape(length, local_heads, HEAD_DIM) / denom_rows[:, :, None]
    grad_num = upstream / denom_rows[:, :, None]
    scalar_grad = -jnp.sum(upstream * attended, axis=2) / denom_rows
    lead_mask = (begins < stretch_start).astype(jnp.float32)
    lead_feat = query_feat * lead_mask[None, None, :]
    lead_state = jnp.einsum("hfl,lhe->hfe", lead_feat, grad_num, precision=HIGHEST)
    lead_norm = jnp.einsum("hfl,lh->hf", lead_feat, scalar_grad, precision=HIGHEST)
    suffix = carried_in(lead_state, lead_norm, has_start, "seq", True)
    grad_blk = grad_num.reshape(blocks, block_len, local_heads, HEAD_DIM)
    scalar_cols = jnp.transpose(scalar_grad.reshape(blocks, block_len, local_heads), (0, 2, 1))
    dscores = jnp.where(
        allowed[:, None],
        jnp.einsum("bthe,bshe->bhts", grad_blk, value_blk, precision=HIGHEST)
        + scalar_cols[:, :, :, None],
        0.0,
    )
    lead_blk = query_blk * from_carry[:, None, None, :]
    lead_states = jnp.einsum("bhft,bthe->bhfe", lead_blk, grad_blk, precision=HIGHEST)
    lead_norms = jnp.einsum("bhft,bht->bhf", lead_blk, scalar_cols, precision=HIGHEST)
    back_state = jnp.einsum("bc,chfe->bhfe", behind_w, lead_states, precision=HIGHEST) + behind_p[
        :, None, None, None
    ] * suffix[0][None]
    back_norm = jnp.einsum("bc,chf->bhf", behind_w, lead_norms, precision=HIGHEST) + behind_p[
        :, None, None
    ] * suffix[1][None]
    grad_qblocks = jnp.einsum("bhts,bhfs->bhft", dscores, key_blk, precision=HIGHEST) + from_carry[
        :, None, None, :
    ] * (
        jnp.einsum("bhfe,bthe->bhft", carry_state, grad_blk, precision=HIGHEST)
        + carry_norm[:, :, :, None] * scalar_cols[:, :, None, :]
    )
    grad_kblocks = jnp.einsum("bhts,bhft->bhfs", dscores, query_blk, precision=HIGHEST) + block_tail[
        :, None, None, :
    ] * (
        jnp.einsum("bhfe,bshe->bhfs", back_state, value_blk, precision=HIGHEST)
        + back_norm[:, :, :, None]
    )
    grad_vblocks = jnp.einsum("bhts,bthe->bshe", scores, grad_blk, precision=HIGHEST) + block_tail[
        :, :, None, None
    ] * jnp.einsum("bhfs,bhfe->bshe", key_blk, back_state, precision=HIGHEST)
    query_grad = jnp.transpose(grad_qblocks, (1, 2, 0, 3)).reshape(local_heads, feat_count, length)
    key_grad = jnp.transpose(grad_kblocks, (1, 2, 0, 3)).reshape(local_heads, feat_count, length)
    value_grad = grad_vblocks.reshape(length, local_heads, HEAD_DIM)
    query_in = jnp.transpose(feature_pull(query_parts, query_grad) * scale_key, (2, 0, 1))
    key_in = jnp.transpose(feature_pull(key_parts, key_grad) * scale_key, (2, 0, 1))
    return jnp.concatenate([query_in, key_in, value_grad], axis=2).reshape(
        length, local_heads * head_width
    )


def summed_everywhere(part, here, axes):
    count = math.prod(lax.axis_size(axis) for axis in axes)
    distance = 1
    while distance < count:
        radix = 4 if count // distance >= 4 else 2
        place = (here // distance) % radix
        got = [part] + [
            lax.ppermute(part, axes, [(s, s ^ (m * distance)) for s in range(count)])
            for m in range(1, radix)
        ]
        members = []
        for q in range(radix):
            value = got[q]
            for p in range(1, radix):
                value = jnp.where(place == p, got[p ^ q], value)
            members.append(value)
        while len(members) > 1:
            members = [members[k] + members[k + 1] for k in range(0, len(members), 2)]
        part = members[0]
        distance *= radix
    return part


def on_device(projected, out_grads, conv_weight, doc_lengths):
    row_count = projected.shape[0]
    head_count = lax.axis_size("head")
    seq_index = lax.axis_index("seq")
    head_index = lax.axis_index("head")
    group_len = row_count * head_count
    token_base = (seq_index * head_count + head_index) * row_count
    stretch_start = seq_index * group_len
    token_begins, token_offsets = doc_place(doc_lengths, token_base, row_count + 2)
    leading = passed_along(projected[row_count - 2 :], ("seq", "head"), 1)
    outgoing = conv_forward(projected, leading, conv_weight, token_offsets)
    arrived, upstream = (
        lax.all_to_all(outgoing, "head", split_axis=1, concat_axis=0, tiled=True),
        lax.all_to_all(out_grads, "head", split_axis=1, concat_axis=0, tiled=True),
    )
    group_begins, group_offsets = doc_place(doc_lengths, stretch_start, group_len + 2)
    grad_mixed = attention_grads(arrived, upstream, group_begins[:group_len], stretch_start)
    returned = lax.all_to_all(grad_mixed, "head", split_axis=0, concat_axis=1, tiled=True)
    trailing = passed_along(returned[:2], ("seq", "head"), -1)
    grad_projected, weight_part = conv_backward(
        returned, trailing, projected, leading, conv_weight, token_offsets
    )
    grad_conv = summed_everywhere(weight_part, seq_index * head_count + head_index, ("seq", "head"))
    return (grad_projected, grad_conv)


def solution(mesh):
    return jax.shard_map(
        on_device,
        mesh=mesh,
        in_specs=(P(("seq", "head"), None), P(("seq", "head"), None), P(), P()),
        out_specs=(P(("seq", "head"), None), P()),
        check_vma=False,
    )
```

```python
import math

import jax
import jax.numpy as jnp
import numpy as np
from jax import lax
from jax.sharding import PartitionSpec as P

KEY_DIM = 16
HEAD_DIM = 128


HIGHEST = lax.Precision.HIGHEST


def carried_in(state, norm, flag, axis, reverse):
    count = lax.axis_size(axis)
    step = -1 if reverse else 1
    size = state.size
    packed = jnp.concatenate([state.reshape(-1), norm.reshape(-1), flag])
    width = 128
    padded = jnp.pad(packed, (0, -packed.shape[0] % width)).reshape(-1, width)
    at_flag = divmod(packed.shape[0] - 1, width)

    def shifted(rows, distance):
        pairs = [(s, s + distance * step) for s in range(count) if 0 <= s + distance * step < count]
        return lax.ppermute(rows, axis, pairs)

    def folded(parts):
        acc = parts[-1]
        for later in reversed(parts[:-1]):
            acc = later + (1.0 - later[at_flag]) * acc
        return acc

    radix = 4
    acc = folded([shifted(padded, k) for k in range(1, radix + 1)])
    window = radix
    while window < count:
        acc = folded([acc] + [shifted(acc, k * window) for k in range(1, radix)])
        window *= radix
    total = acc.reshape(-1)
    return (total[:size].reshape(state.shape), total[size : size + norm.size].reshape(norm.shape))


def passed_along(value, axis, steps):
    count = lax.axis_size(axis)
    initial, last = (max(0, -steps), min(count, count - steps))
    return lax.ppermute(value, axis, [(source, source + steps) for source in range(initial, last)])


def pair_pickers(key_size):
    upper_i, upper_j = np.triu_indices(key_size)
    factors = np.where(upper_i == upper_j, 1.0 / math.sqrt(2.0), 1.0).astype(np.float32)
    eye = np.eye(key_size, dtype=np.float32)
    return (jnp.asarray(eye[upper_i]), jnp.asarray(eye[upper_j]), jnp.asarray(factors))


def feature_map(columns):
    pick_i, pick_j, factors = pair_pickers(columns.shape[1])
    first = jnp.einsum("pk,hkl->hpl", pick_i, columns, precision=HIGHEST)
    second = jnp.einsum("pk,hkl->hpl", pick_j, columns, precision=HIGHEST)
    products = first * second * factors[None, :, None]
    constant = jnp.ones((columns.shape[0], 1, columns.shape[2]), jnp.float32)
    return (jnp.concatenate([constant, columns, products], axis=1), (first, second))


def feature_pull(parts, grad):
    first, second = parts
    key_size = KEY_DIM
    pick_i, pick_j, factors = pair_pickers(key_size)
    pair_grad = grad[:, 1 + key_size :] * factors[None, :, None]
    return (
        grad[:, 1 : 1 + key_size]
        + jnp.einsum("pk,hpl->hkl", pick_i, pair_grad * second, precision=HIGHEST)
        + jnp.einsum("pk,hpl->hkl", pick_j, pair_grad * first, precision=HIGHEST)
    )


def doc_place(doc_lengths, anchor, amount):
    positions = anchor + jnp.arange(amount, dtype=jnp.int32)
    starts = jnp.cumsum(doc_lengths) - doc_lengths
    begins = jnp.max(jnp.where(starts[None, :] <= positions[:, None], starts[None, :], 0), axis=1)
    return (begins, positions - begins)


def conv_forward(signal, leading, weights, offsets):
    row_count = signal.shape[0]
    behind = jnp.concatenate([leading, signal], axis=0)
    back_one = behind[1 : row_count + 1] * (offsets[0:row_count] >= 1).astype(jnp.float32)[:, None]
    back_two = behind[0:row_count] * (offsets[0:row_count] >= 2).astype(jnp.float32)[:, None]
    return weights[0] * signal + weights[1] * back_one + weights[2] * back_two


def conv_backward(grad_rows, trailing, signal, leading, weights, offsets):
    row_count = grad_rows.shape[0]
    ahead_rows = jnp.concatenate([grad_rows, trailing], axis=0)
    ahead_one = (
        ahead_rows[1 : row_count + 1]
        * (offsets[1 : row_count + 1] >= 1).astype(jnp.float32)[:, None]
    )
    ahead_two = (
        ahead_rows[2 : row_count + 2]
        * (offsets[2 : row_count + 2] >= 2).astype(jnp.float32)[:, None]
    )
    grad_signal = weights[0] * grad_rows + weights[1] * ahead_one + weights[2] * ahead_two
    behind = jnp.concatenate([leading, signal], axis=0)
    own_one = (offsets[0:row_count] >= 1).astype(jnp.float32)[:, None]
    own_two = (offsets[0:row_count] >= 2).astype(jnp.float32)[:, None]
    grad_weights = jnp.stack(
        [
            jnp.sum(grad_rows * signal, axis=0),
            jnp.sum(grad_rows * behind[1 : row_count + 1] * own_one, axis=0),
            jnp.sum(grad_rows * behind[0:row_count] * own_two, axis=0),
        ],
        axis=0,
    )
    return (grad_signal, grad_weights)


def attention_grads(mixed_rows, out_flat, begins, stretch_start):
    length = mixed_rows.shape[0]
    head_width = 2 * KEY_DIM + HEAD_DIM
    local_heads = mixed_rows.shape[1] // head_width
    block_len = min(128, length)
    blocks = length // block_len
    scale_key = KEY_DIM ** (-0.25)
    shaped = mixed_rows.reshape(length, local_heads, head_width)
    query_cols = jnp.transpose(shaped[:, :, :KEY_DIM], (1, 2, 0)) * scale_key
    key_cols = jnp.transpose(shaped[:, :, KEY_DIM : 2 * KEY_DIM], (1, 2, 0)) * scale_key
    values = shaped[:, :, 2 * KEY_DIM :]
    upstream = out_flat.reshape(length, local_heads, HEAD_DIM)
    query_feat, query_parts = feature_map(query_cols)
    key_feat, key_parts = feature_map(key_cols)
    feat_count = query_feat.shape[1]
    last_begin = begins[length - 1]
    has_start = (last_begin >= stretch_start).astype(jnp.float32).reshape(1)
    tail_mask = (begins == last_begin).astype(jnp.float32)
    tail_feat = key_feat * tail_mask[None, None, :]
    tail_state = jnp.einsum("hfl,lhe->hfe", tail_feat, values, precision=HIGHEST)
    tail_norm = jnp.sum(tail_feat, axis=2)
    prefix = carried_in(tail_state, tail_norm, has_start, "seq", False)
    causal = jnp.arange(block_len)[:, None] >= jnp.arange(block_len)[None, :]
    query_blk = jnp.transpose(query_feat.reshape(local_heads, feat_count, blocks, block_len), (2, 0, 1, 3))
    key_blk = jnp.transpose(key_feat.reshape(local_heads, feat_count, blocks, block_len), (2, 0, 1, 3))
    value_blk = values.reshape(blocks, block_len, local_heads, HEAD_DIM)
    doc_blk = begins.reshape(blocks, block_len)
    block_start = stretch_start + jnp.arange(blocks, dtype=jnp.int32) * block_len
    allowed = causal[None] & (doc_blk[:, :, None] == doc_blk[:, None, :])
    from_carry = (doc_blk < block_start[:, None]).astype(jnp.float32)
    block_tail = (doc_blk == doc_blk[:, block_len - 1 :]).astype(jnp.float32)
    breaks = (doc_blk[:, block_len - 1] >= block_start).astype(jnp.int32)
    upto = jnp.cumsum(breaks)
    before = upto - breaks
    order = jnp.arange(blocks)
    ahead_w = ((order[None, :] < order[:, None]) & (before[:, None] == upto[None, :])).astype(jnp.float32)
    ahead_p = (before == 0).astype(jnp.float32)
    behind_w = ((order[None, :] > order[:, None]) & (before[None, :] == upto[:, None])).astype(jnp.float32)
    behind_p = (upto[blocks - 1] == upto).astype(jnp.float32)
    scores = jnp.where(
        allowed[:, None], jnp.einsum("bhft,bhfs->bhts", query_blk, key_blk, precision=HIGHEST), 0.0
    )
    tail_keys = key_blk * block_tail[:, None, None, :]
    tail_states = jnp.einsum("bhfs,bshe->bhfe", tail_keys, value_blk, precision=HIGHEST)
    tail_norms = jnp.sum(tail_keys, axis=3)
    carry_state = jnp.einsum("bc,chfe->bhfe", ahead_w, tail_states, precision=HIGHEST) + ahead_p[
        :, None, None, None
    ] * prefix[0][None]
    carry_norm = jnp.einsum("bc,chf->bhf", ahead_w, tail_norms, precision=HIGHEST) + ahead_p[
        :, None, None
    ] * prefix[1][None]
    numerators = jnp.einsum("bhts,bshe->bthe", scores, value_blk, precision=HIGHEST) + from_carry[
        :, :, None, None
    ] * jnp.einsum("bhft,bhfe->bthe", query_blk, carry_state, precision=HIGHEST)
    denominators = jnp.sum(scores, axis=3) + from_carry[:, None, :] * jnp.einsum(
        "bhft,bhf->bht", query_blk, carry_norm, precision=HIGHEST
    )
    denom_rows = jnp.transpose(denominators, (0, 2, 1)).reshape(length, local_heads)
    attended = numerators.reshape(length, local_heads, HEAD_DIM) / denom_rows[:, :, None]
    grad_num = upstream / denom_rows[:, :, None]
    scalar_grad = -jnp.sum(upstream * attended, axis=2) / denom_rows
    lead_mask = (begins < stretch_start).astype(jnp.float32)
    lead_feat = query_feat * lead_mask[None, None, :]
    lead_state = jnp.einsum("hfl,lhe->hfe", lead_feat, grad_num, precision=HIGHEST)
    lead_norm = jnp.einsum("hfl,lh->hf", lead_feat, scalar_grad, precision=HIGHEST)
    suffix = carried_in(lead_state, lead_norm, has_start, "seq", True)
    grad_blk = grad_num.reshape(blocks, block_len, local_heads, HEAD_DIM)
    scalar_cols = jnp.transpose(scalar_grad.reshape(blocks, block_len, local_heads), (0, 2, 1))
    dscores = jnp.where(
        allowed[:, None],
        jnp.einsum("bthe,bshe->bhts", grad_blk, value_blk, precision=HIGHEST)
        + scalar_cols[:, :, :, None],
        0.0,
    )
    lead_blk = query_blk * from_carry[:, None, None, :]
    lead_states = jnp.einsum("bhft,bthe->bhfe", lead_blk, grad_blk, precision=HIGHEST)
    lead_norms = jnp.einsum("bhft,bht->bhf", lead_blk, scalar_cols, precision=HIGHEST)
    back_state = jnp.einsum("bc,chfe->bhfe", behind_w, lead_states, precision=HIGHEST) + behind_p[
        :, None, None, None
    ] * suffix[0][None]
    back_norm = jnp.einsum("bc,chf->bhf", behind_w, lead_norms, precision=HIGHEST) + behind_p[
        :, None, None
    ] * suffix[1][None]
    grad_qblocks = jnp.einsum("bhts,bhfs->bhft", dscores, key_blk, precision=HIGHEST) + from_carry[
        :, None, None, :
    ] * (
        jnp.einsum("bhfe,bthe->bhft", carry_state, grad_blk, precision=HIGHEST)
        + carry_norm[:, :, :, None] * scalar_cols[:, :, None, :]
    )
    grad_kblocks = jnp.einsum("bhts,bhft->bhfs", dscores, query_blk, precision=HIGHEST) + block_tail[
        :, None, None, :
    ] * (
        jnp.einsum("bhfe,bshe->bhfs", back_state, value_blk, precision=HIGHEST)
        + back_norm[:, :, :, None]
    )
    grad_vblocks = jnp.einsum("bhts,bthe->bshe", scores, grad_blk, precision=HIGHEST) + block_tail[
        :, :, None, None
    ] * jnp.einsum("bhfs,bhfe->bshe", key_blk, back_state, precision=HIGHEST)
    query_grad = jnp.transpose(grad_qblocks, (1, 2, 0, 3)).reshape(local_heads, feat_count, length)
    key_grad = jnp.transpose(grad_kblocks, (1, 2, 0, 3)).reshape(local_heads, feat_count, length)
    value_grad = grad_vblocks.reshape(length, local_heads, HEAD_DIM)
    query_in = jnp.transpose(feature_pull(query_parts, query_grad) * scale_key, (2, 0, 1))
    key_in = jnp.transpose(feature_pull(key_parts, key_grad) * scale_key, (2, 0, 1))
    return jnp.concatenate([query_in, key_in, value_grad], axis=2).reshape(
        length, local_heads * head_width
    )


def summed_everywhere(part, here, axes):
    count = math.prod(lax.axis_size(axis) for axis in axes)
    distance = 1
    while distance < count:
        radix = min(8, count // distance)
        place = (here // distance) % radix
        got = [part] + [
            lax.ppermute(part, axes, [(s, s ^ (m * distance)) for s in range(count)])
            for m in range(1, radix)
        ]
        members = []
        for q in range(radix):
            value = got[q]
            for p in range(1, radix):
                value = jnp.where(place == p, got[p ^ q], value)
            members.append(value)
        while len(members) > 1:
            members = [members[k] + members[k + 1] for k in range(0, len(members), 2)]
        part = members[0]
        distance *= radix
    return part


def on_device(projected, out_grads, conv_weight, doc_lengths):
    row_count = projected.shape[0]
    head_count = lax.axis_size("head")
    seq_index = lax.axis_index("seq")
    head_index = lax.axis_index("head")
    group_len = row_count * head_count
    token_base = (seq_index * head_count + head_index) * row_count
    stretch_start = seq_index * group_len
    token_begins, token_offsets = doc_place(doc_lengths, token_base, row_count + 2)
    leading = passed_along(projected[row_count - 2 :], ("seq", "head"), 1)
    outgoing = conv_forward(projected, leading, conv_weight, token_offsets)
    arrived, upstream = (
        lax.all_to_all(outgoing, "head", split_axis=1, concat_axis=0, tiled=True),
        lax.all_to_all(out_grads, "head", split_axis=1, concat_axis=0, tiled=True),
    )
    group_begins, group_offsets = doc_place(doc_lengths, stretch_start, group_len + 2)
    grad_mixed = attention_grads(arrived, upstream, group_begins[:group_len], stretch_start)
    returned = lax.all_to_all(grad_mixed, "head", split_axis=0, concat_axis=1, tiled=True)
    trailing = passed_along(returned[:2], ("seq", "head"), -1)
    grad_projected, weight_part = conv_backward(
        returned, trailing, projected, leading, conv_weight, token_offsets
    )
    grad_conv = summed_everywhere(weight_part, seq_index * head_count + head_index, ("seq", "head"))
    return (grad_projected, grad_conv)


def solution(mesh):
    return jax.shard_map(
        on_device,
        mesh=mesh,
        in_specs=(P(("seq", "head"), None), P(("seq", "head"), None), P(), P()),
        out_specs=(P(("seq", "head"), None), P()),
        check_vma=False,
    )
```

```python
import math

import jax
import jax.numpy as jnp
import numpy as np
from jax import lax
from jax.sharding import PartitionSpec as P

KEY_DIM = 16
HEAD_DIM = 128


HIGHEST = lax.Precision.HIGHEST


def carried_in(state, norm, flag, axis, reverse):
    count = lax.axis_size(axis)
    step = -1 if reverse else 1
    size = state.size
    packed = jnp.concatenate([state.reshape(-1), norm.reshape(-1), flag])
    width = 128
    padded = jnp.pad(packed, (0, -packed.shape[0] % width)).reshape(-1, width)
    at_flag = divmod(packed.shape[0] - 1, width)

    def shifted(rows, distance):
        pairs = [(s, s + distance * step) for s in range(count) if 0 <= s + distance * step < count]
        return lax.ppermute(rows, axis, pairs)

    acc = shifted(padded, 1)
    distance = 1
    if count > 2:
        second = shifted(padded, 2)
        acc = acc + (1.0 - acc[at_flag]) * second
        distance = 2
    while distance < count:
        earlier = shifted(acc, distance)
        acc = acc + (1.0 - acc[at_flag]) * earlier
        distance *= 2
    total = acc.reshape(-1)
    return (total[:size].reshape(state.shape), total[size : size + norm.size].reshape(norm.shape))


def passed_along(value, axis, steps):
    count = lax.axis_size(axis)
    initial, last = (max(0, -steps), min(count, count - steps))
    return lax.ppermute(value, axis, [(source, source + steps) for source in range(initial, last)])


def pair_pickers(key_size):
    upper_i, upper_j = np.triu_indices(key_size)
    factors = np.where(upper_i == upper_j, 1.0 / math.sqrt(2.0), 1.0).astype(np.float32)
    eye = np.eye(key_size, dtype=np.float32)
    return (jnp.asarray(eye[upper_i]), jnp.asarray(eye[upper_j]), jnp.asarray(factors))


def feature_map(columns):
    pick_i, pick_j, factors = pair_pickers(columns.shape[1])
    first = jnp.einsum("pk,hkl->hpl", pick_i, columns, precision=HIGHEST)
    second = jnp.einsum("pk,hkl->hpl", pick_j, columns, precision=HIGHEST)
    products = first * second * factors[None, :, None]
    constant = jnp.ones((columns.shape[0], 1, columns.shape[2]), jnp.float32)
    return (jnp.concatenate([constant, columns, products], axis=1), (first, second))


def feature_pull(parts, grad):
    first, second = parts
    key_size = KEY_DIM
    pick_i, pick_j, factors = pair_pickers(key_size)
    pair_grad = grad[:, 1 + key_size :] * factors[None, :, None]
    return (
        grad[:, 1 : 1 + key_size]
        + jnp.einsum("pk,hpl->hkl", pick_i, pair_grad * second, precision=HIGHEST)
        + jnp.einsum("pk,hpl->hkl", pick_j, pair_grad * first, precision=HIGHEST)
    )


def doc_place(doc_lengths, anchor, amount):
    positions = anchor + jnp.arange(amount, dtype=jnp.int32)
    starts = jnp.cumsum(doc_lengths) - doc_lengths
    begins = jnp.max(jnp.where(starts[None, :] <= positions[:, None], starts[None, :], 0), axis=1)
    return (begins, positions - begins)


def conv_forward(signal, leading, weights, offsets):
    row_count = signal.shape[0]
    behind = jnp.concatenate([leading, signal], axis=0)
    back_one = behind[1 : row_count + 1] * (offsets[0:row_count] >= 1).astype(jnp.float32)[:, None]
    back_two = behind[0:row_count] * (offsets[0:row_count] >= 2).astype(jnp.float32)[:, None]
    return weights[0] * signal + weights[1] * back_one + weights[2] * back_two


def conv_backward(grad_rows, trailing, signal, leading, weights, offsets):
    row_count = grad_rows.shape[0]
    ahead_rows = jnp.concatenate([grad_rows, trailing], axis=0)
    ahead_one = (
        ahead_rows[1 : row_count + 1]
        * (offsets[1 : row_count + 1] >= 1).astype(jnp.float32)[:, None]
    )
    ahead_two = (
        ahead_rows[2 : row_count + 2]
        * (offsets[2 : row_count + 2] >= 2).astype(jnp.float32)[:, None]
    )
    grad_signal = weights[0] * grad_rows + weights[1] * ahead_one + weights[2] * ahead_two
    behind = jnp.concatenate([leading, signal], axis=0)
    own_one = (offsets[0:row_count] >= 1).astype(jnp.float32)[:, None]
    own_two = (offsets[0:row_count] >= 2).astype(jnp.float32)[:, None]
    grad_weights = jnp.stack(
        [
            jnp.sum(grad_rows * signal, axis=0),
            jnp.sum(grad_rows * behind[1 : row_count + 1] * own_one, axis=0),
            jnp.sum(grad_rows * behind[0:row_count] * own_two, axis=0),
        ],
        axis=0,
    )
    return (grad_signal, grad_weights)


def attention_grads(mixed_rows, out_flat, begins, stretch_start):
    length = mixed_rows.shape[0]
    head_width = 2 * KEY_DIM + HEAD_DIM
    local_heads = mixed_rows.shape[1] // head_width
    block_len = min(128, length)
    blocks = length // block_len
    scale_key = KEY_DIM ** (-0.25)
    shaped = mixed_rows.reshape(length, local_heads, head_width)
    query_cols = jnp.transpose(shaped[:, :, :KEY_DIM], (1, 2, 0)) * scale_key
    key_cols = jnp.transpose(shaped[:, :, KEY_DIM : 2 * KEY_DIM], (1, 2, 0)) * scale_key
    values = shaped[:, :, 2 * KEY_DIM :]
    upstream = out_flat.reshape(length, local_heads, HEAD_DIM)
    query_feat, query_parts = feature_map(query_cols)
    key_feat, key_parts = feature_map(key_cols)
    feat_count = query_feat.shape[1]
    last_begin = begins[length - 1]
    has_start = (last_begin >= stretch_start).astype(jnp.float32).reshape(1)
    tail_mask = (begins == last_begin).astype(jnp.float32)
    tail_feat = key_feat * tail_mask[None, None, :]
    tail_state = jnp.einsum("hfl,lhe->hfe", tail_feat, values, precision=HIGHEST)
    tail_norm = jnp.sum(tail_feat, axis=2)
    prefix = carried_in(tail_state, tail_norm, has_start, "seq", False)
    causal = jnp.arange(block_len)[:, None] >= jnp.arange(block_len)[None, :]
    query_blk = jnp.transpose(query_feat.reshape(local_heads, feat_count, blocks, block_len), (2, 0, 1, 3))
    key_blk = jnp.transpose(key_feat.reshape(local_heads, feat_count, blocks, block_len), (2, 0, 1, 3))
    value_blk = values.reshape(blocks, block_len, local_heads, HEAD_DIM)
    doc_blk = begins.reshape(blocks, block_len)
    block_start = stretch_start + jnp.arange(blocks, dtype=jnp.int32) * block_len
    allowed = causal[None] & (doc_blk[:, :, None] == doc_blk[:, None, :])
    from_carry = (doc_blk < block_start[:, None]).astype(jnp.float32)
    block_tail = (doc_blk == doc_blk[:, block_len - 1 :]).astype(jnp.float32)
    breaks = (doc_blk[:, block_len - 1] >= block_start).astype(jnp.int32)
    upto = jnp.cumsum(breaks)
    before = upto - breaks
    order = jnp.arange(blocks)
    ahead_w = ((order[None, :] < order[:, None]) & (before[:, None] == upto[None, :])).astype(jnp.float32)
    ahead_p = (before == 0).astype(jnp.float32)
    behind_w = ((order[None, :] > order[:, None]) & (before[None, :] == upto[:, None])).astype(jnp.float32)
    behind_p = (upto[blocks - 1] == upto).astype(jnp.float32)
    scores = jnp.where(
        allowed[:, None], jnp.einsum("bhft,bhfs->bhts", query_blk, key_blk, precision=HIGHEST), 0.0
    )
    tail_keys = key_blk * block_tail[:, None, None, :]
    tail_states = jnp.einsum("bhfs,bshe->bhfe", tail_keys, value_blk, precision=HIGHEST)
    tail_norms = jnp.sum(tail_keys, axis=3)
    carry_state = jnp.einsum("bc,chfe->bhfe", ahead_w, tail_states, precision=HIGHEST) + ahead_p[
        :, None, None, None
    ] * prefix[0][None]
    carry_norm = jnp.einsum("bc,chf->bhf", ahead_w, tail_norms, precision=HIGHEST) + ahead_p[
        :, None, None
    ] * prefix[1][None]
    numerators = jnp.einsum("bhts,bshe->bthe", scores, value_blk, precision=HIGHEST) + from_carry[
        :, :, None, None
    ] * jnp.einsum("bhft,bhfe->bthe", query_blk, carry_state, precision=HIGHEST)
    denominators = jnp.sum(scores, axis=3) + from_carry[:, None, :] * jnp.einsum(
        "bhft,bhf->bht", query_blk, carry_norm, precision=HIGHEST
    )
    denom_rows = jnp.transpose(denominators, (0, 2, 1)).reshape(length, local_heads)
    attended = numerators.reshape(length, local_heads, HEAD_DIM) / denom_rows[:, :, None]
    grad_num = upstream / denom_rows[:, :, None]
    scalar_grad = -jnp.sum(upstream * attended, axis=2) / denom_rows
    lead_mask = (begins < stretch_start).astype(jnp.float32)
    lead_feat = query_feat * lead_mask[None, None, :]
    lead_state = jnp.einsum("hfl,lhe->hfe", lead_feat, grad_num, precision=HIGHEST)
    lead_norm = jnp.einsum("hfl,lh->hf", lead_feat, scalar_grad, precision=HIGHEST)
    suffix = carried_in(lead_state, lead_norm, has_start, "seq", True)
    grad_blk = grad_num.reshape(blocks, block_len, local_heads, HEAD_DIM)
    scalar_cols = jnp.transpose(scalar_grad.reshape(blocks, block_len, local_heads), (0, 2, 1))
    dscores = jnp.where(
        allowed[:, None],
        jnp.einsum("bthe,bshe->bhts", grad_blk, value_blk, precision=HIGHEST)
        + scalar_cols[:, :, :, None],
        0.0,
    )
    lead_blk = query_blk * from_carry[:, None, None, :]
    lead_states = jnp.einsum("bhft,bthe->bhfe", lead_blk, grad_blk, precision=HIGHEST)
    lead_norms = jnp.einsum("bhft,bht->bhf", lead_blk, scalar_cols, precision=HIGHEST)
    back_state = jnp.einsum("bc,chfe->bhfe", behind_w, lead_states, precision=HIGHEST) + behind_p[
        :, None, None, None
    ] * suffix[0][None]
    back_norm = jnp.einsum("bc,chf->bhf", behind_w, lead_norms, precision=HIGHEST) + behind_p[
        :, None, None
    ] * suffix[1][None]
    grad_qblocks = jnp.einsum("bhts,bhfs->bhft", dscores, key_blk, precision=HIGHEST) + from_carry[
        :, None, None, :
    ] * (
        jnp.einsum("bhfe,bthe->bhft", carry_state, grad_blk, precision=HIGHEST)
        + carry_norm[:, :, :, None] * scalar_cols[:, :, None, :]
    )
    grad_kblocks = jnp.einsum("bhts,bhft->bhfs", dscores, query_blk, precision=HIGHEST) + block_tail[
        :, None, None, :
    ] * (
        jnp.einsum("bhfe,bshe->bhfs", back_state, value_blk, precision=HIGHEST)
        + back_norm[:, :, :, None]
    )
    grad_vblocks = jnp.einsum("bhts,bthe->bshe", scores, grad_blk, precision=HIGHEST) + block_tail[
        :, :, None, None
    ] * jnp.einsum("bhfs,bhfe->bshe", key_blk, back_state, precision=HIGHEST)
    query_grad = jnp.transpose(grad_qblocks, (1, 2, 0, 3)).reshape(local_heads, feat_count, length)
    key_grad = jnp.transpose(grad_kblocks, (1, 2, 0, 3)).reshape(local_heads, feat_count, length)
    value_grad = grad_vblocks.reshape(length, local_heads, HEAD_DIM)
    query_in = jnp.transpose(feature_pull(query_parts, query_grad) * scale_key, (2, 0, 1))
    key_in = jnp.transpose(feature_pull(key_parts, key_grad) * scale_key, (2, 0, 1))
    return jnp.concatenate([query_in, key_in, value_grad], axis=2).reshape(
        length, local_heads * head_width
    )


def summed_everywhere(part, here, axes):
    count = math.prod(lax.axis_size(axis) for axis in axes)
    distance = 1
    while distance < count:
        radix = 4 if count // distance >= 4 else 2
        place = (here // distance) % radix
        got = [part] + [
            lax.ppermute(part, axes, [(s, s ^ (m * distance)) for s in range(count)])
            for m in range(1, radix)
        ]
        members = []
        for q in range(radix):
            value = got[q]
            for p in range(1, radix):
                value = jnp.where(place == p, got[p ^ q], value)
            members.append(value)
        while len(members) > 1:
            members = [members[k] + members[k + 1] for k in range(0, len(members), 2)]
        part = members[0]
        distance *= radix
    return part


def on_device(projected, out_grads, conv_weight, doc_lengths):
    row_count = projected.shape[0]
    head_count = lax.axis_size("head")
    seq_index = lax.axis_index("seq")
    head_index = lax.axis_index("head")
    group_len = row_count * head_count
    token_base = (seq_index * head_count + head_index) * row_count
    stretch_start = seq_index * group_len
    token_begins, token_offsets = doc_place(doc_lengths, token_base, row_count + 2)
    leading = passed_along(projected[row_count - 2 :], ("seq", "head"), 1)
    outgoing = conv_forward(projected, leading, conv_weight, token_offsets)
    mixed_width = outgoing.shape[1] // head_count
    both = jnp.concatenate(
        [outgoing.reshape(row_count, head_count, -1), out_grads.reshape(row_count, head_count, -1)],
        axis=2,
    ).reshape(row_count, -1)
    landed = lax.all_to_all(both, "head", split_axis=1, concat_axis=0, tiled=True)
    arrived, upstream = (landed[:, :mixed_width], landed[:, mixed_width:])
    group_begins, group_offsets = doc_place(doc_lengths, stretch_start, group_len + 2)
    grad_mixed = attention_grads(arrived, upstream, group_begins[:group_len], stretch_start)
    returned = lax.all_to_all(grad_mixed, "head", split_axis=0, concat_axis=1, tiled=True)
    trailing = passed_along(returned[:2], ("seq", "head"), -1)
    grad_projected, weight_part = conv_backward(
        returned, trailing, projected, leading, conv_weight, token_offsets
    )
    grad_conv = summed_everywhere(weight_part, seq_index * head_count + head_index, ("seq", "head"))
    return (grad_projected, grad_conv)


def solution(mesh):
    return jax.shard_map(
        on_device,
        mesh=mesh,
        in_specs=(P(("seq", "head"), None), P(("seq", "head"), None), P(), P()),
        out_specs=(P(("seq", "head"), None), P()),
        check_vma=False,
    )
```
